512 devices in a mesh: req: 8 (over z_lo), row: 8 (over x, core), col: 8 (over y, z_hi).
Axes of the slice: x: 4, y: 4, z: 16 (z_hi: 2, z_lo: 8; z = z_hi * 8 + z_lo), core: 2. Of those that a mesh axis runs over, the one named last changes fastest.
Arguments:
- tokens: bfloat16 [1792, 32768], P('col', ('req', 'row')), may hold values from -6 to 6
- qkv_weight: bfloat16 [1792, 2304], P('col', 'row'), may hold values from -0.125 to 0.125
- out_weight: bfloat16 [1792, 1792], P('row', 'col'), may hold values from -0.125 to 0.125
- head_gain: float32 [1792], P('row'), may hold values from 0.1 to 1.9
- prefix_keys: bfloat16 [24, 256, 8192], P('req', 'row', 'col'), may hold values from -6 to 6
- prefix_values: bfloat16 [24, 1792, 8192], P('req', 'row', 'col'), may hold values from -6 to 6
- suffix_len: int32 [64], P(('req', 'col')), may hold values from 1 to 512, 24576 in all
- prefix_owner: int32 [64], P(('req', 'col')), may hold values from 0 to 23
Outputs:
- layer_out: bfloat16 [1792, 32768], P('col', ('req', 'row'))
The draws below stay inside these ranges and needn't reach their ends.
Inputs may be any that keep to these rules, and one draw needn't show every extreme that they name: `suffix_len`: the longest suffix has exactly 512 live tokens.
All inputs are finite; a program needn't handle non-finite values. No bound on the sum of `suffix_len` on one device may be relied on, other than what follows from the above.
Results may differ from the reference program's by a relative error of at most 0.015.
Values may be sent and summed in bfloat16 or wider, within the bound.
No kernel may reach another device: no remote copies, remote signals or barrier semaphores. Data moves between devices by JAX's collectives and lax.ppermute only.
A program may use at most 64 MiB of HBM per device.

```python
import math
import jax
import jax.numpy as jnp
import numpy as np
from jax import lax

D = 1792
H = 16
FEAT = 16
PLEN = 8192
SLOTS = 512
HD = 112
PREFIXES = 24
REQS = 64
TOKENS = 32768
N_ROW = 8
N_COL = 8


def plant(drawn, key, low, high):
    longest = drawn.shape.index(max(drawn.shape))
    spots = []
    for shift in (0, 1):
        where = [jax.random.randint(jax.random.fold_in(key, axis), (), 0, length) for axis, length in enumerate(drawn.shape)]
        where[longest] = (where[longest] + shift) % drawn.shape[longest]
        spots.append(tuple(where))
    return drawn.at[spots[0]].set(low).at[spots[1]].set(high)


def block_scale(stream_key, shape, shards, least, high):
    loudness, own = 1.0, jax.random.fold_in(stream_key, 6)
    for dim, parts in shards:
        heights = jnp.exp(jax.random.uniform(jax.random.fold_in(own, dim), (parts,), jnp.float32, least / len(shards), high / len(shards)))
        loudness = loudness * jnp.repeat(heights, shape[dim] // parts).reshape([-1 if axis == dim else 1 for axis in range(len(shape))])
    return loudness


def split_up(amount, total, reach, lean):
    weights = [(1 << 20) // math.isqrt(standing ** lean) + 1 for standing in range(2, amount + 1)]
    spare, counts = total - reach - (amount - 1), [1] * (amount - 1)
    while spare > 0:
        candidates = [i for i in range(amount - 1) if counts[i] < reach]
        whole, remaining = sum([weights[i] for i in candidates]), spare
        for i in candidates:
            extra = min(reach - counts[i], max(1, remaining * weights[i] // whole), spare)
            counts[i] = counts[i] + extra
            spare = spare - extra
    return np.array([reach] + counts)


def ragged_sizes(rng, amount, total, limit, slope):
    if amount == 2:
        one = jax.random.randint(rng, (), max(1, total - limit), min(limit, total - 1) + 1)
        return jnp.stack([one, total - one])
    sizes = jnp.asarray(split_up(amount, total, limit, slope), jnp.int32)
    couples = (amount - 1) // 2
    giver, sink = sizes[1:1 + 2 * couples:2], sizes[2:2 + 2 * couples:2]
    slack = jnp.minimum(giver - 1, limit - sink)
    moved = jax.random.randint(jax.random.fold_in(rng, 1), (couples,), 0, 1 << 20) % (slack + 1)
    sizes = sizes.at[1:1 + 2 * couples:2].set(giver - moved).at[2:2 + 2 * couples:2].set(sink + moved)
    return sizes[jax.random.permutation(jax.random.fold_in(rng, 2), amount)]


def noise(own_key, extent, width, reach, cuts=(), held_as=jnp.bfloat16):
    gain = block_scale(own_key, extent, cuts, -0.22, 0.18) if cuts else 1.0
    drawn = jax.random.normal(own_key, extent, jnp.float32) * width * gain
    return jnp.minimum(jnp.maximum(drawn, -reach), reach).astype(held_as)


def setup_inputs(seed: int = 0) -> dict:
    keys = jax.random.split(jax.random.key(seed), 9)
    return {
        "tokens": noise(keys[0], (D, TOKENS), 1.0, 6.0, ((0, 8), (1, 64))),
        "qkv_weight": noise(keys[1], (D, H * (2 * FEAT + HD)), D ** -0.5, 0.125, ((0, 8), (1, 8))),
        "out_weight": noise(keys[2], (D, D), D ** -0.5, 0.125, ((0, 8), (1, 8))),
        "head_gain": jnp.clip(1.0 + 0.18 * jax.random.normal(keys[3], (D,), jnp.float32), 0.1, 1.9),
        "prefix_keys": noise(keys[4], (PREFIXES, H * FEAT, PLEN), 1.0, 6.0, ((0, 8), (1, 8), (2, 8))),
        "prefix_values": noise(keys[5], (PREFIXES, D, PLEN), 1.0, 6.0, ((0, 8), (1, 8), (2, 8))),
        "suffix_len": ragged_sizes(keys[6], REQS, REQS * SLOTS * 3 // 4, SLOTS, 2).astype(jnp.int32),
        "prefix_owner": plant(jax.random.randint(keys[7], (REQS,), 0, PREFIXES), jax.random.fold_in(keys[7], 1), 0, PREFIXES - 1).astype(jnp.int32),
    }


epsilon = 1e-05

def feature_map(values_in):
    feature_count = values_in.shape[-1]
    squares = (values_in[..., :, None] * values_in[..., None, :]).reshape(values_in.shape[:-1] + (feature_count * feature_count,))
    constant = jnp.ones(values_in.shape[:-1] + (1,), jnp.float32)
    linear = values_in * feature_count ** (-0.25)
    quadratic = squares * (0.5 ** 0.5 / feature_count ** 0.5)
    return jnp.concatenate([constant, linear, quadratic], axis=-1).astype(jnp.bfloat16)

def feature_columns(values_in):
    feature_count = values_in.shape[-2]
    length = values_in.shape[-1]
    squares = (values_in[..., :, None, :] * values_in[..., None, :, :]).reshape(values_in.shape[:-2] + (feature_count * feature_count, length))
    constant = jnp.ones(values_in.shape[:-2] + (1, length), jnp.float32)
    linear = values_in * feature_count ** (-0.25)
    quadratic = squares * (0.5 ** 0.5 / feature_count ** 0.5)
    return jnp.concatenate([constant, linear, quadratic], axis=-2).astype(jnp.bfloat16)

def reference(tokens, qkv_weight, out_weight, head_gain, prefix_keys, prefix_values, suffix_len, prefix_owner):
    row_width = 2 * FEAT + HD
    block_width = D // N_COL
    token_rows = tokens.T
    summed = jnp.zeros((TOKENS, H * row_width), jnp.float32)
    for column_index in range(N_COL):
        partial_sum = jnp.dot(token_rows[:, column_index * block_width:(column_index + 1) * block_width], qkv_weight[column_index * block_width:(column_index + 1) * block_width], preferred_element_type=jnp.float32)
        summed = summed + lax.optimization_barrier(partial_sum.astype(jnp.bfloat16)).astype(jnp.float32)
    projected = summed.astype(jnp.bfloat16).reshape(REQS, SLOTS, H, row_width)

    def one_state(cache_pair):
        keys_cached, values_cached = cache_pair
        feats = feature_columns(keys_cached.reshape(H, FEAT, PLEN).astype(jnp.float32))
        return jnp.einsum('het,hvt->hev', feats.astype(jnp.float32), values_cached.reshape(H, HD, PLEN).astype(jnp.float32))
    states = lax.map(one_state, (prefix_keys, prefix_values))
    gains = head_gain.reshape(H, HD).astype(jnp.float32)

    def one_request(request_item):
        block_rows, length, prefix_pick = request_item
        queries = block_rows[..., :FEAT]
        keys_now = block_rows[..., FEAT:2 * FEAT]
        values_now = block_rows[..., 2 * FEAT:]
        chosen = lax.dynamic_index_in_dim(states, prefix_pick, 0, keepdims=False)
        feats_query = feature_map(queries.astype(jnp.float32)).astype(jnp.float32)
        carried = jnp.einsum('the,hev->thv', feats_query, chosen, precision=lax.Precision.HIGHEST)
        scores = jnp.einsum('thf,shf->hts', queries.astype(jnp.float32), keys_now.astype(jnp.float32))
        weights = 1.0 + scores * FEAT ** (-0.5) + scores * scores * (0.5 / FEAT)
        positions = jnp.arange(SLOTS, dtype=jnp.int32)
        allowed = (positions[None, :] <= positions[:, None]) & (positions[None, :] < length)
        weights = jnp.where(allowed[None], weights, 0.0).astype(jnp.bfloat16)
        within = jnp.einsum('hts,shv->thv', weights.astype(jnp.float32), values_now.astype(jnp.float32))
        active = (positions < length)[:, None, None]
        attended = jnp.where(active, carried + within, 0.0)
        inverse_rms = lax.rsqrt(lax.optimization_barrier(jnp.mean(attended * attended, axis=-1, keepdims=True)) + epsilon)
        normed = attended * inverse_rms * gains
        return normed.astype(jnp.bfloat16).reshape(SLOTS, D)
    hidden = lax.map(one_request, (projected, suffix_len, prefix_owner)).reshape(TOKENS, D)
    row_block = D // N_ROW
    result = token_rows.astype(jnp.float32)
    for row_index in range(N_ROW):
        partial_sum = jnp.dot(hidden[:, row_index * row_block:(row_index + 1) * row_block], out_weight[row_index * row_block:(row_index + 1) * row_block], preferred_element_type=jnp.float32)
        result = result + lax.optimization_barrier(partial_sum.astype(jnp.bfloat16)).astype(jnp.float32)
    return result.astype(jnp.bfloat16).T
```

```python
import jax
import jax.numpy as jnp
import numpy as np
from jax import lax
from jax.sharding import Mesh, PartitionSpec as P

FEAT = 16
SLOTS = 512
HD = 112

ROW = ("x", "c")
COL = ("y", "zh")

epsilon = 1e-05


def feature_map(values_in):
    feature_count = values_in.shape[-1]
    squares = (values_in[..., :, None] * values_in[..., None, :]).reshape(
        values_in.shape[:-1] + (feature_count * feature_count,)
    )
    constant = jnp.ones(values_in.shape[:-1] + (1,), jnp.float32)
    linear = values_in * feature_count ** (-0.25)
    quadratic = squares * (0.5**0.5 / feature_count**0.5)
    return jnp.concatenate([constant, linear, quadratic], axis=-1).astype(jnp.bfloat16)


def feature_columns(values_in):
    feature_count = values_in.shape[-2]
    length = values_in.shape[-1]
    squares = (values_in[..., :, None, :] * values_in[..., None, :, :]).reshape(
        values_in.shape[:-2] + (feature_count * feature_count, length)
    )
    constant = jnp.ones(values_in.shape[:-2] + (1, length), jnp.float32)
    linear = values_in * feature_count ** (-0.25)
    quadratic = squares * (0.5**0.5 / feature_count**0.5)
    return jnp.concatenate([constant, linear, quadratic], axis=-2).astype(jnp.bfloat16)


def shards(
    tokens, qkv_weight, out_weight, head_gain, prefix_keys, prefix_values, suffix_len, prefix_owner
):
    n_col = lax.psum(1, COL)
    heads_here = head_gain.shape[0] // HD
    partial_proj = lax.dot_general(
        lax.all_gather(tokens, ROW, axis=1, tiled=True),
        qkv_weight,
        (((0,), (0,)), ((), ())),
        preferred_element_type=jnp.float32,
    ).astype(jnp.bfloat16)
    projected = lax.psum_scatter(partial_proj, "y", scatter_dimension=0, tiled=True)
    projected = lax.psum_scatter(projected, "zh", scatter_dimension=0, tiled=True)
    projected = projected.reshape(SLOTS, heads_here, 2 * FEAT + HD)
    queries = projected[..., :FEAT]
    keys_now = projected[..., FEAT : 2 * FEAT]
    values_now = projected[..., 2 * FEAT :]

    pref_here = prefix_keys.shape[0]
    plen_here = prefix_keys.shape[2]
    feats_cached = feature_columns(
        prefix_keys.reshape(pref_here, heads_here, FEAT, plen_here).astype(jnp.float32)
    )
    values_cached = prefix_values.reshape(pref_here, heads_here, HD, plen_here)
    partial_state = jnp.einsum(
        "phet,phvt->phev", feats_cached, values_cached, preferred_element_type=jnp.float32
    )
    state_shape = partial_state.shape[1:]
    piece = partial_state[0].size // n_col
    pieces = partial_state.astype(jnp.bfloat16).reshape(pref_here, n_col, piece)
    pieces = jnp.swapaxes(pieces, 0, 1)
    pieces = lax.psum_scatter(pieces, "y", scatter_dimension=0, tiled=True)
    pieces = lax.psum_scatter(pieces, "zh", scatter_dimension=0, tiled=True)
    pieces = lax.all_gather(pieces[0], "req", axis=0, tiled=True)
    owners = lax.all_gather(prefix_owner, COL, axis=0, tiled=True)
    to_send = jnp.take(pieces, owners, axis=0)
    chosen = lax.all_to_all(to_send, COL, 0, 0, tiled=True)
    chosen = chosen.reshape(state_shape).astype(jnp.float32)

    feats_query = feature_map(queries.astype(jnp.float32)).astype(jnp.float32)
    carried = jnp.einsum("the,hev->thv", feats_query, chosen, precision=lax.Precision.HIGHEST)
    scores = jnp.einsum("thf,shf->hts", queries, keys_now, preferred_element_type=jnp.float32)
    weights = 1.0 + scores * FEAT ** (-0.5) + scores * scores * (0.5 / FEAT)
    positions = jnp.arange(SLOTS, dtype=jnp.int32)
    length = suffix_len[0]
    allowed = (positions[None, :] <= positions[:, None]) & (positions[None, :] < length)
    weights = jnp.where(allowed[None], weights, 0.0).astype(jnp.bfloat16)
    within = jnp.einsum("hts,shv->thv", weights, values_now, preferred_element_type=jnp.float32)
    active = (positions < length)[:, None, None]
    attended = jnp.where(active, carried + within, 0.0)
    inverse_rms = lax.rsqrt(jnp.mean(attended * attended, axis=-1, keepdims=True) + epsilon)
    gains = head_gain.reshape(heads_here, HD)
    normed = (attended * inverse_rms * gains).astype(jnp.bfloat16).reshape(SLOTS, heads_here * HD)
    gathered = lax.all_gather(normed, "zh", axis=0, tiled=True)
    gathered = lax.all_gather(gathered, "y", axis=0, tiled=True)
    out_terms = lax.dot_general(
        out_weight,
        gathered,
        (((0,), (1,)), ((), ())),
        preferred_element_type=jnp.float32,
    )
    mixed_sums = lax.psum_scatter(
        out_terms.astype(jnp.bfloat16), ROW, scatter_dimension=1, tiled=True
    ).astype(jnp.float32)
    return (tokens.astype(jnp.float32) + mixed_sums).astype(jnp.bfloat16)


def solution(mesh):
    n_req, n_row, n_col = (mesh.shape[a] for a in ("req", "row", "col"))
    fine = Mesh(
        np.asarray(mesh.devices).reshape(n_req, n_row // 2, 2, n_col // 2, 2),
        ("req", "x", "c", "y", "zh"),
    )
    in_specs = (
        P(COL, ("req",) + ROW),
        P(COL, ROW),
        P(ROW, COL),
        P(ROW),
        P("req", ROW, COL),
        P("req", ROW, COL),
        P(("req",) + COL),
        P(("req",) + COL),
    )
    out_specs = P(COL, ("req",) + ROW)
    return jax.shard_map(shards, mesh=fine, in_specs=in_specs, out_specs=out_specs, check_vma=False)
```

```python
import jax
import jax.numpy as jnp
import numpy as np
from jax import lax
from jax.sharding import Mesh, PartitionSpec as P

FEAT = 16
SLOTS = 512
HD = 112

ROW = ("x", "c")
COL = ("y", "zh")

epsilon = 1e-05


def feature_map(values_in):
    feature_count = values_in.shape[-1]
    squares = (values_in[..., :, None] * values_in[..., None, :]).reshape(
        values_in.shape[:-1] + (feature_count * feature_count,)
    )
    constant = jnp.ones(values_in.shape[:-1] + (1,), jnp.float32)
    linear = values_in * feature_count ** (-0.25)
    quadratic = squares * (0.5**0.5 / feature_count**0.5)
    return jnp.concatenate([constant, linear, quadratic], axis=-1).astype(jnp.bfloat16)


def feature_columns(values_in):
    feature_count = values_in.shape[-2]
    length = values_in.shape[-1]
    squares = (values_in[..., :, None, :] * values_in[..., None, :, :]).reshape(
        values_in.shape[:-2] + (feature_count * feature_count, length)
    )
    constant = jnp.ones(values_in.shape[:-2] + (1, length), jnp.float32)
    linear = values_in * feature_count ** (-0.25)
    quadratic = squares * (0.5**0.5 / feature_count**0.5)
    return jnp.concatenate([constant, linear, quadratic], axis=-2).astype(jnp.bfloat16)


def shards(
    tokens, qkv_weight, out_weight, head_gain, prefix_keys, prefix_values, suffix_len, prefix_owner
):
    n_row = lax.psum(1, ROW)
    n_col = lax.psum(1, COL)
    heads_here = head_gain.shape[0] // HD
    row_here = lax.axis_index("x") * 2 + lax.axis_index("c")
    col_here = lax.axis_index("y") * 2 + lax.axis_index("zh")
    lens = lax.all_gather(suffix_len, COL, axis=0, tiled=True)
    owners = lax.all_gather(prefix_owner, COL, axis=0, tiled=True)

    pref_here = prefix_keys.shape[0]
    plen_here = prefix_keys.shape[2]
    feats_cached = feature_columns(
        prefix_keys.reshape(pref_here, heads_here, FEAT, plen_here).astype(jnp.float32)
    )
    values_cached = prefix_values.reshape(pref_here, heads_here, HD, plen_here)
    partial_state = jnp.einsum(
        "phet,phvt->phev", feats_cached, values_cached, preferred_element_type=jnp.float32
    )
    state_shape = partial_state.shape[1:]
    piece = partial_state[0].size // n_col
    pieces = partial_state.astype(jnp.bfloat16).reshape(pref_here, n_col, piece)
    pieces = lax.all_to_all(jnp.swapaxes(pieces, 0, 1), COL, 0, 0, tiled=True)
    pieces = jnp.sum(pieces.astype(jnp.float32), axis=0).astype(jnp.bfloat16)
    pieces = lax.all_gather(pieces, "req", axis=0, tiled=True)
    to_send = jnp.take(pieces, owners, axis=0)
    chosen = lax.all_to_all(to_send, COL, 0, 0, tiled=True)
    flat = ROW + COL
    perm = [(i * n_col + j, j * n_col + i) for i in range(n_row) for j in range(n_col)]
    chosen = lax.ppermute(chosen, flat, perm)
    chosen = chosen.reshape(state_shape).astype(jnp.float32)

    weight_all = lax.all_gather(qkv_weight, ROW, axis=1, tiled=True)
    partial_proj = lax.dot_general(
        weight_all, tokens, (((0,), (0,)), ((), ())), preferred_element_type=jnp.float32
    ).astype(jnp.bfloat16)
    projected = lax.psum_scatter(partial_proj, "y", scatter_dimension=0, tiled=True)
    projected = lax.psum_scatter(projected, "zh", scatter_dimension=0, tiled=True)
    projected = projected.T.reshape(SLOTS, heads_here, 2 * FEAT + HD)
    queries = projected[..., :FEAT]
    keys_now = projected[..., FEAT : 2 * FEAT]
    values_now = projected[..., 2 * FEAT :]

    feats_query = feature_map(queries.astype(jnp.float32)).astype(jnp.float32)
    carried = jnp.einsum("the,hev->thv", feats_query, chosen, precision=lax.Precision.HIGHEST)
    scores = jnp.einsum("thf,shf->hts", queries, keys_now, preferred_element_type=jnp.float32)
    weights = 1.0 + scores * FEAT ** (-0.5) + scores * scores * (0.5 / FEAT)
    positions = jnp.arange(SLOTS, dtype=jnp.int32)
    length = lens[row_here]
    allowed = (positions[None, :] <= positions[:, None]) & (positions[None, :] < length)
    weights = jnp.where(allowed[None], weights, 0.0).astype(jnp.bfloat16)
    within = jnp.einsum("hts,shv->thv", weights, values_now, preferred_element_type=jnp.float32)
    active = (positions < length)[:, None, None]
    attended = jnp.where(active, carried + within, 0.0)
    inverse_rms = lax.rsqrt(jnp.mean(attended * attended, axis=-1, keepdims=True) + epsilon)
    gains_all = lax.all_gather(head_gain, ROW, axis=0, tiled=True)
    gains = lax.dynamic_slice_in_dim(gains_all, col_here * heads_here * HD, heads_here * HD)
    gains = gains.reshape(heads_here, HD)
    normed = (attended * inverse_rms * gains).astype(jnp.bfloat16).reshape(SLOTS, heads_here * HD)
    hidden = lax.all_gather(normed, "zh", axis=0)
    hidden = lax.all_gather(hidden, "y", axis=0)
    hidden = hidden.reshape((n_col,) + normed.shape)
    out_w = lax.all_gather(out_weight, ROW, axis=0, tiled=True)
    out_w = out_w.reshape(n_col, heads_here * HD, out_w.shape[1])
    blocks = jnp.einsum("ktd,kde->ket", hidden, out_w, preferred_element_type=jnp.float32)
    mixed_sums = jnp.sum(blocks.astype(jnp.bfloat16).astype(jnp.float32), axis=0)
    return (tokens.astype(jnp.float32) + mixed_sums).astype(jnp.bfloat16)


def solution(mesh):
    n_req, n_row, n_col = (mesh.shape[a] for a in ("req", "row", "col"))
    fine = Mesh(
        np.asarray(mesh.devices).reshape(n_req, n_row // 2, 2, n_col // 2, 2),
        ("req", "x", "c", "y", "zh"),
    )
    in_specs = (
        P(COL, ("req",) + ROW),
        P(COL, ROW),
        P(ROW, COL),
        P(ROW),
        P("req", ROW, COL),
        P("req", ROW, COL),
        P(("req",) + COL),
        P(("req",) + COL),
    )
    out_specs = P(COL, ("req",) + ROW)
    return jax.shard_map(shards, mesh=fine, in_specs=in_specs, out_specs=out_specs, check_vma=False)
```

```python
import jax
import jax.numpy as jnp
import numpy as np
from jax import lax
from jax.sharding import Mesh, PartitionSpec as P

FEAT = 16
SLOTS = 512
HD = 112

ROW = ("x", "c")
COL = ("y", "zh")

epsilon = 1e-05


def feature_map(values_in):
    feature_count = values_in.shape[-1]
    squares = (values_in[..., :, None] * values_in[..., None, :]).reshape(
        values_in.shape[:-1] + (feature_count * feature_count,)
    )
    constant = jnp.ones(values_in.shape[:-1] + (1,), jnp.float32)
    linear = values_in * feature_count ** (-0.25)
    quadratic = squares * (0.5**0.5 / feature_count**0.5)
    return jnp.concatenate([constant, linear, quadratic], axis=-1).astype(jnp.bfloat16)


def feature_columns(values_in):
    feature_count = values_in.shape[-2]
    length = values_in.shape[-1]
    squares = (values_in[..., :, None, :] * values_in[..., None, :, :]).reshape(
        values_in.shape[:-2] + (feature_count * feature_count, length)
    )
    constant = jnp.ones(values_in.shape[:-2] + (1, length), jnp.float32)
    linear = values_in * feature_count ** (-0.25)
    quadratic = squares * (0.5**0.5 / feature_count**0.5)
    return jnp.concatenate([constant, linear, quadratic], axis=-2).astype(jnp.bfloat16)


def gather_by_shifts(x, axis, n):
    me = lax.axis_index(axis)
    got = [x] + [lax.ppermute(x, axis, [(i, (i + k) % n) for i in range(n)]) for k in range(1, n)]
    stacked = jnp.stack(got)
    return jnp.take(stacked, (me - jnp.arange(n)) % n, axis=0)


def reduce_scatter_by_shifts(x, axis, n):
    me = lax.axis_index(axis)
    m = x.shape[0] // n
    total = lax.dynamic_slice_in_dim(x, me * m, m).astype(jnp.float32)
    for k in range(1, n):
        part = lax.dynamic_slice_in_dim(x, ((me + k) % n) * m, m)
        total = total + lax.ppermute(part, axis, [(i, (i + k) % n) for i in range(n)]).astype(
            jnp.float32
        )
    return total


def shards(
    tokens, qkv_weight, out_weight, head_gain, prefix_keys, prefix_values, suffix_len, prefix_owner
):
    n_row = lax.psum(1, ROW)
    n_col = lax.psum(1, COL)
    heads_here = head_gain.shape[0] // HD
    row_here = lax.axis_index("x") * 2 + lax.axis_index("c")
    col_here = lax.axis_index("y") * 2 + lax.axis_index("zh")
    meta = jnp.concatenate([suffix_len, prefix_owner])
    meta = gather_by_shifts(gather_by_shifts(meta, "zh", 2), "y", n_col // 2)
    meta = meta.reshape(n_col, 2)
    lens = meta[:, 0]
    owners = meta[:, 1]
    flat = ROW + COL
    perm = [(i * n_col + j, j * n_col + i) for i in range(n_row) for j in range(n_col)]

    pref_here = prefix_keys.shape[0]
    plen_here = prefix_keys.shape[2]
    feats_cached = feature_columns(
        prefix_keys.reshape(pref_here, heads_here, FEAT, plen_here).astype(jnp.float32)
    )
    values_cached = prefix_values.reshape(pref_here, heads_here, HD, plen_here)
    partial_state = jnp.einsum(
        "phet,phvt->phev", feats_cached, values_cached, preferred_element_type=jnp.float32
    )
    state_shape = partial_state.shape[1:]
    piece = partial_state[0].size // n_col
    pieces = partial_state.astype(jnp.bfloat16).reshape(pref_here, n_col, piece)
    pieces = lax.all_to_all(jnp.swapaxes(pieces, 0, 1), COL, 0, 0, tiled=True)
    pieces = jnp.sum(pieces.astype(jnp.float32), axis=0).astype(jnp.bfloat16)
    pieces = gather_by_shifts(pieces, "req", lax.psum(1, "req"))
    pieces = pieces.reshape((-1, piece))
    to_send = jnp.take(pieces, owners, axis=0)
    chosen = lax.all_to_all(to_send, COL, 0, 0, tiled=True)
    chosen = lax.ppermute(chosen, flat, perm)
    chosen = chosen.reshape(state_shape).astype(jnp.float32)

    weight_all = gather_by_shifts(gather_by_shifts(qkv_weight, "c", 2), "x", n_row // 2)
    weight_all = weight_all.reshape((n_row,) + qkv_weight.shape)
    partial_proj = jnp.einsum(
        "kdj,dt->kjt", weight_all, tokens, preferred_element_type=jnp.float32
    ).astype(jnp.bfloat16)
    partial_proj = partial_proj.reshape(-1, tokens.shape[1])
    projected = reduce_scatter_by_shifts(partial_proj, "y", n_col // 2).astype(jnp.bfloat16)
    projected = reduce_scatter_by_shifts(projected, "zh", 2).astype(jnp.bfloat16)
    projected = projected.T.reshape(SLOTS, heads_here, 2 * FEAT + HD)
    queries = projected[..., :FEAT]
    keys_now = projected[..., FEAT : 2 * FEAT]
    values_now = projected[..., 2 * FEAT :]

    feats_query = feature_map(queries.astype(jnp.float32)).astype(jnp.float32)
    carried = jnp.einsum("the,hev->thv", feats_query, chosen, precision=lax.Precision.HIGHEST)
    scores = jnp.einsum("thf,shf->hts", queries, keys_now, preferred_element_type=jnp.float32)
    weights = 1.0 + scores * FEAT ** (-0.5) + scores * scores * (0.5 / FEAT)
    positions = jnp.arange(SLOTS, dtype=jnp.int32)
    length = lens[row_here]
    allowed = (positions[None, :] <= positions[:, None]) & (positions[None, :] < length)
    weights = jnp.where(allowed[None], weights, 0.0).astype(jnp.bfloat16)
    within = jnp.einsum("hts,shv->thv", weights, values_now, preferred_element_type=jnp.float32)
    active = (positions < length)[:, None, None]
    attended = jnp.where(active, carried + within, 0.0)
    inverse_rms = lax.rsqrt(jnp.mean(attended * attended, axis=-1, keepdims=True) + epsilon)
    gains = lax.ppermute(head_gain, flat, perm).reshape(heads_here, HD)
    normed = (attended * inverse_rms * gains).astype(jnp.bfloat16).reshape(SLOTS, heads_here * HD)
    hidden = gather_by_shifts(gather_by_shifts(normed, "zh", 2), "y", n_col // 2)
    hidden = hidden.reshape((n_col,) + normed.shape)
    out_w = gather_by_shifts(gather_by_shifts(out_weight, "c", 2), "x", n_row // 2)
    out_w = out_w.reshape((n_row,) + out_weight.shape)
    blocks = jnp.einsum("ktd,kde->ket", hidden, out_w, preferred_element_type=jnp.float32)
    mixed_sums = jnp.sum(blocks.astype(jnp.bfloat16).astype(jnp.float32), axis=0)
    return (tokens.astype(jnp.float32) + mixed_sums).astype(jnp.bfloat16)


def solution(mesh):
    n_req, n_row, n_col = (mesh.shape[a] for a in ("req", "row", "col"))
    fine = Mesh(
        np.asarray(mesh.devices).reshape(n_req, n_row // 2, 2, n_col // 2, 2),
        ("req", "x", "c", "y", "zh"),
    )
    in_specs = (
        P(COL, ("req",) + ROW),
        P(COL, ROW),
        P(ROW, COL),
        P(ROW),
        P("req", ROW, COL),
        P("req", ROW, COL),
        P(("req",) + COL),
        P(("req",) + COL),
    )
    out_specs = P(COL, ("req",) + ROW)
    return jax.shard_map(shards, mesh=fine, in_specs=in_specs, out_specs=out_specs, check_vma=False)
```

```python
import jax
import jax.numpy as jnp
import numpy as np
from jax import lax
from jax.sharding import Mesh, PartitionSpec as P

FEAT = 16
SLOTS = 512
HD = 112

ROW = ("x", "c")
COL = ("y", "zh")

epsilon = 1e-05


def feature_map(values_in):
    feature_count = values_in.shape[-1]
    squares = (values_in[..., :, None] * values_in[..., None, :]).reshape(
        values_in.shape[:-1] + (feature_count * feature_count,)
    )
    constant = jnp.ones(values_in.shape[:-1] + (1,), jnp.float32)
    linear = values_in * feature_count ** (-0.25)
    quadratic = squares * (0.5**0.5 / feature_count**0.5)
    return jnp.concatenate([constant, linear, quadratic], axis=-1).astype(jnp.bfloat16)


def feature_columns(values_in):
    feature_count = values_in.shape[-2]
    length = values_in.shape[-1]
    squares = (values_in[..., :, None, :] * values_in[..., None, :, :]).reshape(
        values_in.shape[:-2] + (feature_count * feature_count, length)
    )
    constant = jnp.ones(values_in.shape[:-2] + (1, length), jnp.float32)
    linear = values_in * feature_count ** (-0.25)
    quadratic = squares * (0.5**0.5 / feature_count**0.5)
    return jnp.concatenate([constant, linear, quadratic], axis=-2).astype(jnp.bfloat16)


def gather_by_shifts(x, axis, n):
    me = lax.axis_index(axis)
    got = [x] + [lax.ppermute(x, axis, [(i, (i + k) % n) for i in range(n)]) for k in range(1, n)]
    stacked = jnp.stack(got)
    return jnp.take(stacked, (me - jnp.arange(n)) % n, axis=0)


def reduce_scatter_by_shifts(x, axis, n):
    me = lax.axis_index(axis)
    m = x.shape[0] // n
    total = lax.dynamic_slice_in_dim(x, me * m, m).astype(jnp.float32)
    for k in range(1, n):
        part = lax.dynamic_slice_in_dim(x, ((me + k) % n) * m, m)
        total = total + lax.ppermute(part, axis, [(i, (i + k) % n) for i in range(n)]).astype(
            jnp.float32
        )
    return total


def shards(
    tokens, qkv_weight, out_weight, head_gain, prefix_keys, prefix_values, suffix_len, prefix_owner
):
    n_row = lax.psum(1, ROW)
    n_col = lax.psum(1, COL)
    heads_here = head_gain.shape[0] // HD
    row_here = lax.axis_index("x") * 2 + lax.axis_index("c")
    col_here = lax.axis_index("y") * 2 + lax.axis_index("zh")
    flat = ROW + COL
    perm = [(i * n_col + j, j * n_col + i) for i in range(n_row) for j in range(n_col)]

    pref_here = prefix_keys.shape[0]
    plen_here = prefix_keys.shape[2]
    feats_cached = feature_columns(
        prefix_keys.reshape(pref_here, heads_here, FEAT, plen_here).astype(jnp.float32)
    )
    values_cached = prefix_values.reshape(pref_here, heads_here, HD, plen_here)
    partial_state = jnp.einsum(
        "phet,phvt->phev", feats_cached, values_cached, preferred_element_type=jnp.float32
    )
    state_shape = partial_state.shape[1:]
    piece = partial_state[0].size // n_col
    pieces = partial_state.astype(jnp.bfloat16).reshape(pref_here, n_col, piece)
    pieces = jnp.swapaxes(pieces, 0, 1).reshape(n_col, pref_here * piece)
    meta = jnp.stack([prefix_owner[0], suffix_len[0] // 16, suffix_len[0] % 16])
    meta = jnp.broadcast_to(meta.astype(jnp.bfloat16)[None], (n_col, 3))
    got = lax.all_to_all(jnp.concatenate([pieces, meta], axis=1), COL, 0, 0, tiled=True)
    meta = got[:, pref_here * piece :].astype(jnp.int32)
    owners = meta[:, 0]
    lens = meta[:, 1] * 16 + meta[:, 2]
    pieces = got[:, : pref_here * piece].reshape(n_col, pref_here, piece)
    pieces = jnp.sum(pieces.astype(jnp.float32), axis=0).astype(jnp.bfloat16)
    n_req = lax.psum(1, "req")
    pieces = jnp.broadcast_to(pieces[None], (n_req,) + pieces.shape)
    pieces = lax.all_to_all(pieces, "req", 0, 0, tiled=True)
    pieces = pieces.reshape((-1, piece))
    to_send = jnp.take(pieces, owners, axis=0)
    chosen = lax.all_to_all(to_send, COL, 0, 0, tiled=True)
    chosen = lax.ppermute(chosen, flat, perm)
    chosen = chosen.reshape(state_shape).astype(jnp.float32)

    weight_all = gather_by_shifts(gather_by_shifts(qkv_weight, "c", 2), "x", n_row // 2)
    weight_all = weight_all.reshape((n_row,) + qkv_weight.shape)
    partial_proj = jnp.einsum(
        "kdj,dt->kjt", weight_all, tokens, preferred_element_type=jnp.float32
    ).astype(jnp.bfloat16)
    partial_proj = partial_proj.reshape(-1, tokens.shape[1])
    partial_proj, to_send = lax.optimization_barrier((partial_proj, to_send))
    projected = reduce_scatter_by_shifts(partial_proj, "y", n_col // 2).astype(jnp.bfloat16)
    projected, chosen = lax.optimization_barrier((projected, chosen))
    projected = reduce_scatter_by_shifts(projected, "zh", 2).astype(jnp.bfloat16)
    projected = projected.T.reshape(SLOTS, heads_here, 2 * FEAT + HD)
    queries = projected[..., :FEAT]
    keys_now = projected[..., FEAT : 2 * FEAT]
    values_now = projected[..., 2 * FEAT :]

    feats_query = feature_map(queries.astype(jnp.float32)).astype(jnp.float32)
    carried = jnp.einsum("the,hev->thv", feats_query, chosen, precision=lax.Precision.HIGHEST)
    scores = jnp.einsum("thf,shf->hts", queries, keys_now, preferred_element_type=jnp.float32)
    weights = 1.0 + scores * FEAT ** (-0.5) + scores * scores * (0.5 / FEAT)
    positions = jnp.arange(SLOTS, dtype=jnp.int32)
    length = lens[row_here]
    allowed = (positions[None, :] <= positions[:, None]) & (positions[None, :] < length)
    weights = jnp.where(allowed[None], weights, 0.0).astype(jnp.bfloat16)
    within = jnp.einsum("hts,shv->thv", weights, values_now, preferred_element_type=jnp.float32)
    active = (positions < length)[:, None, None]
    attended = jnp.where(active, carried + within, 0.0)
    inverse_rms = lax.rsqrt(jnp.mean(attended * attended, axis=-1, keepdims=True) + epsilon)
    gains = lax.ppermute(head_gain, flat, perm).reshape(heads_here, HD)
    normed = (attended * inverse_rms * gains).astype(jnp.bfloat16).reshape(SLOTS, heads_here * HD)
    hidden = gather_by_shifts(gather_by_shifts(normed, "zh", 2), "y", n_col // 2)
    hidden = hidden.reshape((n_col,) + normed.shape)
    out_w = gather_by_shifts(gather_by_shifts(out_weight, "c", 2), "x", n_row // 2)
    out_w = out_w.reshape((n_row,) + out_weight.shape)
    blocks = jnp.einsum("ktd,kde->ket", hidden, out_w, preferred_element_type=jnp.float32)
    mixed_sums = jnp.sum(blocks.astype(jnp.bfloat16).astype(jnp.float32), axis=0)
    return (tokens.astype(jnp.float32) + mixed_sums).astype(jnp.bfloat16)


def solution(mesh):
    n_req, n_row, n_col = (mesh.shape[a] for a in ("req", "row", "col"))
    fine = Mesh(
        np.asarray(mesh.devices).reshape(n_req, n_row // 2, 2, n_col // 2, 2),
        ("req", "x", "c", "y", "zh"),
    )
    in_specs = (
        P(COL, ("req",) + ROW),
        P(COL, ROW),
        P(ROW, COL),
        P(ROW),
        P("req", ROW, COL),
        P("req", ROW, COL),
        P(("req",) + COL),
        P(("req",) + COL),
    )
    out_specs = P(COL, ("req",) + ROW)
    return jax.shard_map(shards, mesh=fine, in_specs=in_specs, out_specs=out_specs, check_vma=False)
```

```python
import jax
import jax.numpy as jnp
import numpy as np
from jax import lax
from jax.sharding import Mesh, PartitionSpec as P

FEAT = 16
SLOTS = 512
HD = 112

ROW = ("x", "c")
COL = ("y", "zh")

epsilon = 1e-05


def feature_map(values_in):
    feature_count = values_in.shape[-1]
    squares = (values_in[..., :, None] * values_in[..., None, :]).reshape(
        values_in.shape[:-1] + (feature_count * feature_count,)
    )
    constant = jnp.ones(values_in.shape[:-1] + (1,), jnp.float32)
    linear = values_in * feature_count ** (-0.25)
    quadratic = squares * (0.5**0.5 / feature_count**0.5)
    return jnp.concatenate([constant, linear, quadratic], axis=-1).astype(jnp.bfloat16)


def feature_columns(values_in):
    feature_count = values_in.shape[-2]
    length = values_in.shape[-1]
    squares = (values_in[..., :, None, :] * values_in[..., None, :, :]).reshape(
        values_in.shape[:-2] + (feature_count * feature_count, length)
    )
    constant = jnp.ones(values_in.shape[:-2] + (1, length), jnp.float32)
    linear = values_in * feature_count ** (-0.25)
    quadratic = squares * (0.5**0.5 / feature_count**0.5)
    return jnp.concatenate([constant, linear, quadratic], axis=-2).astype(jnp.bfloat16)


def gather_by_shifts(x, axis, n):
    me = lax.axis_index(axis)
    got = [x] + [lax.ppermute(x, axis, [(i, (i + k) % n) for i in range(n)]) for k in range(1, n)]
    stacked = jnp.stack(got)
    return jnp.take(stacked, (me - jnp.arange(n)) % n, axis=0)


def reduce_scatter_by_shifts(x, axis, n):
    me = lax.axis_index(axis)
    m = x.shape[0] // n
    total = lax.dynamic_slice_in_dim(x, me * m, m).astype(jnp.float32)
    for k in range(1, n):
        part = lax.dynamic_slice_in_dim(x, ((me + k) % n) * m, m)
        total = total + lax.ppermute(part, axis, [(i, (i + k) % n) for i in range(n)]).astype(
            jnp.float32
        )
    return total


def gather_by_all_to_all(x, axis, n):
    return lax.all_to_all(jnp.broadcast_to(x[None], (n,) + x.shape), axis, 0, 0, tiled=True)


def reduce_scatter_by_all_to_all(x, axis, n):
    got = lax.all_to_all(x.reshape((n, x.shape[0] // n) + x.shape[1:]), axis, 0, 0, tiled=True)
    return jnp.sum(got.astype(jnp.float32), axis=0)


def shards(
    tokens, qkv_weight, out_weight, head_gain, prefix_keys, prefix_values, suffix_len, prefix_owner
):
    n_row = lax.psum(1, ROW)
    n_col = lax.psum(1, COL)
    heads_here = head_gain.shape[0] // HD
    row_here = lax.axis_index("x") * 2 + lax.axis_index("c")
    col_here = lax.axis_index("y") * 2 + lax.axis_index("zh")
    flat = ROW + COL
    perm = [(i * n_col + j, j * n_col + i) for i in range(n_row) for j in range(n_col)]

    pref_here = prefix_keys.shape[0]
    plen_here = prefix_keys.shape[2]
    feats_cached = feature_columns(
        prefix_keys.reshape(pref_here, heads_here, FEAT, plen_here).astype(jnp.float32)
    )
    values_cached = prefix_values.reshape(pref_here, heads_here, HD, plen_here)
    partial_state = jnp.einsum(
        "phet,phvt->phev", feats_cached, values_cached, preferred_element_type=jnp.float32
    )
    state_shape = partial_state.shape[1:]
    piece = partial_state[0].size // n_col
    pieces = partial_state.astype(jnp.bfloat16).reshape(pref_here, n_col, piece)
    pieces = jnp.swapaxes(pieces, 0, 1).reshape(n_col, pref_here * piece)
    meta = jnp.stack([prefix_owner[0], suffix_len[0] // 16, suffix_len[0] % 16])
    meta = jnp.broadcast_to(meta.astype(jnp.bfloat16)[None], (n_col, 3))
    got = lax.all_to_all(jnp.concatenate([pieces, meta], axis=1), COL, 0, 0, tiled=True)
    meta = got[:, pref_here * piece :].astype(jnp.int32)
    owners = meta[:, 0]
    lens = meta[:, 1] * 16 + meta[:, 2]
    pieces = got[:, : pref_here * piece].reshape(n_col, pref_here, piece)
    pieces = jnp.sum(pieces.astype(jnp.float32), axis=0).astype(jnp.bfloat16)
    n_req = lax.psum(1, "req")
    pieces = jnp.broadcast_to(pieces[None], (n_req,) + pieces.shape)
    pieces = lax.all_to_all(pieces, "req", 0, 0, tiled=True)
    pieces = pieces.reshape((-1, piece))
    to_send = jnp.take(pieces, owners, axis=0)
    chosen = lax.all_to_all(to_send, COL, 0, 0, tiled=True)
    chosen = lax.ppermute(chosen, flat, perm)
    chosen = chosen.reshape(state_shape).astype(jnp.float32)

    weight_all = gather_by_all_to_all(qkv_weight, ROW, n_row)
    out_w = gather_by_all_to_all(out_weight, ROW, n_row)
    gains = lax.ppermute(head_gain, flat, perm)
    partial_proj = jnp.einsum(
        "kdj,dt->kjt", weight_all, tokens, preferred_element_type=jnp.float32
    ).astype(jnp.bfloat16)
    partial_proj = partial_proj.reshape(-1, tokens.shape[1])
    partial_proj, chosen, out_w, gains = lax.optimization_barrier(
        (partial_proj, chosen, out_w, gains)
    )
    projected = reduce_scatter_by_all_to_all(partial_proj, "y", n_col // 2).astype(jnp.bfloat16)
    projected = reduce_scatter_by_shifts(projected, "zh", 2).astype(jnp.bfloat16)
    projected = projected.T.reshape(SLOTS, heads_here, 2 * FEAT + HD)
    queries = projected[..., :FEAT]
    keys_now = projected[..., FEAT : 2 * FEAT]
    values_now = projected[..., 2 * FEAT :]

    feats_query = feature_map(queries.astype(jnp.float32)).astype(jnp.float32)
    carried = jnp.einsum("the,hev->thv", feats_query, chosen, precision=lax.Precision.HIGHEST)
    scores = jnp.einsum("thf,shf->hts", queries, keys_now, preferred_element_type=jnp.float32)
    weights = 1.0 + scores * FEAT ** (-0.5) + scores * scores * (0.5 / FEAT)
    positions = jnp.arange(SLOTS, dtype=jnp.int32)
    length = lens[row_here]
    allowed = (positions[None, :] <= positions[:, None]) & (positions[None, :] < length)
    weights = jnp.where(allowed[None], weights, 0.0).astype(jnp.bfloat16)
    within = jnp.einsum("hts,shv->thv", weights, values_now, preferred_element_type=jnp.float32)
    active = (positions < length)[:, None, None]
    attended = jnp.where(active, carried + within, 0.0)
    inverse_rms = lax.rsqrt(jnp.mean(attended * attended, axis=-1, keepdims=True) + epsilon)
    gains = gains.reshape(heads_here, HD)
    normed = (attended * inverse_rms * gains).astype(jnp.bfloat16).reshape(SLOTS, heads_here * HD)
    hidden = gather_by_all_to_all(gather_by_shifts(normed, "zh", 2), "y", n_col // 2)
    hidden = hidden.reshape((n_col,) + normed.shape)
    blocks = jnp.einsum("ktd,kde->ket", hidden, out_w, preferred_element_type=jnp.float32)
    mixed_sums = jnp.sum(blocks.astype(jnp.bfloat16).astype(jnp.float32), axis=0)
    return (tokens.astype(jnp.float32) + mixed_sums).astype(jnp.bfloat16)


def solution(mesh):
    n_req, n_row, n_col = (mesh.shape[a] for a in ("req", "row", "col"))
    fine = Mesh(
        np.asarray(mesh.devices).reshape(n_req, n_row // 2, 2, n_col // 2, 2),
        ("req", "x", "c", "y", "zh"),
    )
    in_specs = (
        P(COL, ("req",) + ROW),
        P(COL, ROW),
        P(ROW, COL),
        P(ROW),
        P("req", ROW, COL),
        P("req", ROW, COL),
        P(("req",) + COL),
        P(("req",) + COL),
    )
    out_specs = P(COL, ("req",) + ROW)
    return jax.shard_map(shards, mesh=fine, in_specs=in_specs, out_specs=out_specs, check_vma=False)
```

```python
import jax
import jax.numpy as jnp
import numpy as np
from jax import lax
from jax.sharding import Mesh, PartitionSpec as P

FEAT = 16
SLOTS = 512
HD = 112

ROW = ("x", "c")
COL = ("y", "zh")

epsilon = 1e-05


def feature_map(values_in):
    feature_count = values_in.shape[-1]
    squares = (values_in[..., :, None] * values_in[..., None, :]).reshape(
        values_in.shape[:-1] + (feature_count * feature_count,)
    )
    constant = jnp.ones(values_in.shape[:-1] + (1,), jnp.float32)
    linear = values_in * feature_count ** (-0.25)
    quadratic = squares * (0.5**0.5 / feature_count**0.5)
    return jnp.concatenate([constant, linear, quadratic], axis=-1).astype(jnp.bfloat16)


def feature_columns(values_in):
    feature_count = values_in.shape[-2]
    length = values_in.shape[-1]
    squares = (values_in[..., :, None, :] * values_in[..., None, :, :]).reshape(
        values_in.shape[:-2] + (feature_count * feature_count, length)
    )
    constant = jnp.ones(values_in.shape[:-2] + (1, length), jnp.float32)
    linear = values_in * feature_count ** (-0.25)
    quadratic = squares * (0.5**0.5 / feature_count**0.5)
    return jnp.concatenate([constant, linear, quadratic], axis=-2).astype(jnp.bfloat16)


def gather_by_shifts(x, axis, n):
    me = lax.axis_index(axis)
    got = [x] + [lax.ppermute(x, axis, [(i, (i + k) % n) for i in range(n)]) for k in range(1, n)]
    stacked = jnp.stack(got)
    return jnp.take(stacked, (me - jnp.arange(n)) % n, axis=0)


def reduce_scatter_by_shifts(x, axis, n):
    me = lax.axis_index(axis)
    m = x.shape[0] // n
    total = lax.dynamic_slice_in_dim(x, me * m, m).astype(jnp.float32)
    for k in range(1, n):
        part = lax.dynamic_slice_in_dim(x, ((me + k) % n) * m, m)
        total = total + lax.ppermute(part, axis, [(i, (i + k) % n) for i in range(n)]).astype(
            jnp.float32
        )
    return total


def shards(
    tokens, qkv_weight, out_weight, head_gain, prefix_keys, prefix_values, suffix_len, prefix_owner
):
    n_row = lax.psum(1, ROW)
    n_col = lax.psum(1, COL)
    heads_here = head_gain.shape[0] // HD
    row_here = lax.axis_index("x") * 2 + lax.axis_index("c")
    col_here = lax.axis_index("y") * 2 + lax.axis_index("zh")
    flat = ROW + COL
    perm = [(i * n_col + j, j * n_col + i) for i in range(n_row) for j in range(n_col)]

    pref_here = prefix_keys.shape[0]
    plen_here = prefix_keys.shape[2]
    feats_cached = feature_columns(
        prefix_keys.reshape(pref_here, heads_here, FEAT, plen_here).astype(jnp.float32)
    )
    values_cached = prefix_values.reshape(pref_here, heads_here, HD, plen_here)
    partial_state = jnp.einsum(
        "phet,phvt->phev", feats_cached, values_cached, preferred_element_type=jnp.float32
    )
    state_shape = partial_state.shape[1:]
    piece = partial_state[0].size // n_col
    pieces = partial_state.astype(jnp.bfloat16).reshape(pref_here, n_col, piece)
    pieces = jnp.swapaxes(pieces, 0, 1).reshape(n_col, pref_here * piece)
    meta = jnp.stack([prefix_owner[0], suffix_len[0] // 16, suffix_len[0] % 16])
    meta = jnp.broadcast_to(meta.astype(jnp.bfloat16)[None], (n_col, 3))
    got = lax.all_to_all(jnp.concatenate([pieces, meta], axis=1), COL, 0, 0, tiled=True)
    meta = got[:, pref_here * piece :].astype(jnp.int32)
    owners = meta[:, 0]
    lens = meta[:, 1] * 16 + meta[:, 2]
    pieces = got[:, : pref_here * piece].reshape(n_col, pref_here, piece)
    pieces = jnp.sum(pieces.astype(jnp.float32), axis=0).astype(jnp.bfloat16)
    n_req = lax.psum(1, "req")
    pieces = jnp.broadcast_to(pieces[None], (n_req,) + pieces.shape)
    pieces = lax.all_to_all(pieces, "req", 0, 0, tiled=True)
    pieces = pieces.reshape((-1, piece))
    to_send = jnp.take(pieces, owners, axis=0)
    chosen = lax.all_to_all(to_send, COL, 0, 0, tiled=True)
    chosen = lax.ppermute(chosen, flat, perm)
    chosen = chosen.reshape(state_shape).astype(jnp.float32)

    both = jnp.concatenate([qkv_weight, out_weight], axis=1)
    both = gather_by_shifts(gather_by_shifts(both, "c", 2), "x", n_row // 2)
    both = both.reshape((n_row,) + both.shape[2:])
    weight_all = both[:, :, : qkv_weight.shape[1]]
    out_w = both[:, :, qkv_weight.shape[1] :]
    partial_proj = jnp.einsum(
        "kdj,dt->kjt", weight_all, tokens, preferred_element_type=jnp.float32
    ).astype(jnp.bfloat16)
    partial_proj = partial_proj.reshape(-1, tokens.shape[1])
    partial_proj, to_send = lax.optimization_barrier((partial_proj, to_send))
    projected = reduce_scatter_by_shifts(partial_proj, "y", n_col // 2).astype(jnp.bfloat16)
    projected, chosen = lax.optimization_barrier((projected, chosen))
    projected = reduce_scatter_by_shifts(projected, "zh", 2).astype(jnp.bfloat16)
    projected = projected.T.reshape(SLOTS, heads_here, 2 * FEAT + HD)
    queries = projected[..., :FEAT]
    keys_now = projected[..., FEAT : 2 * FEAT]
    values_now = projected[..., 2 * FEAT :]

    feats_query = feature_map(queries.astype(jnp.float32)).astype(jnp.float32)
    carried = jnp.einsum("the,hev->thv", feats_query, chosen, precision=lax.Precision.HIGHEST)
    scores = jnp.einsum("thf,shf->hts", queries, keys_now, preferred_element_type=jnp.float32)
    weights = 1.0 + scores * FEAT ** (-0.5) + scores * scores * (0.5 / FEAT)
    positions = jnp.arange(SLOTS, dtype=jnp.int32)
    length = lens[row_here]
    allowed = (positions[None, :] <= positions[:, None]) & (positions[None, :] < length)
    weights = jnp.where(allowed[None], weights, 0.0).astype(jnp.bfloat16)
    within = jnp.einsum("hts,shv->thv", weights, values_now, preferred_element_type=jnp.float32)
    active = (positions < length)[:, None, None]
    attended = jnp.where(active, carried + within, 0.0)
    inverse_rms = lax.rsqrt(jnp.mean(attended * attended, axis=-1, keepdims=True) + epsilon)
    gains = lax.ppermute(head_gain, flat, perm).reshape(heads_here, HD)
    normed = (attended * inverse_rms * gains).astype(jnp.bfloat16).reshape(SLOTS, heads_here * HD)
    hidden = gather_by_shifts(gather_by_shifts(normed, "zh", 2), "y", n_col // 2)
    hidden = hidden.reshape((n_col,) + normed.shape)
    blocks = jnp.einsum("ktd,kde->ket", hidden, out_w, preferred_element_type=jnp.float32)
    mixed_sums = jnp.sum(blocks.astype(jnp.bfloat16).astype(jnp.float32), axis=0)
    return (tokens.astype(jnp.float32) + mixed_sums).astype(jnp.bfloat16)


def solution(mesh):
    n_req, n_row, n_col = (mesh.shape[a] for a in ("req", "row", "col"))
    fine = Mesh(
        np.asarray(mesh.devices).reshape(n_req, n_row // 2, 2, n_col // 2, 2),
        ("req", "x", "c", "y", "zh"),
    )
    in_specs = (
        P(COL, ("req",) + ROW),
        P(COL, ROW),
        P(ROW, COL),
        P(ROW),
        P("req", ROW, COL),
        P("req", ROW, COL),
        P(("req",) + COL),
        P(("req",) + COL),
    )
    out_specs = P(COL, ("req",) + ROW)
    return jax.shard_map(shards, mesh=fine, in_specs=in_specs, out_specs=out_specs, check_vma=False)
```

```python
import jax
import jax.numpy as jnp
import numpy as np
from jax import lax
from jax.sharding import Mesh, PartitionSpec as P

FEAT = 16
SLOTS = 512
HD = 112

ROW = ("x", "c")
COL = ("y", "zh")

epsilon = 1e-05


def feature_map(values_in):
    feature_count = values_in.shape[-1]
    squares = (values_in[..., :, None] * values_in[..., None, :]).reshape(
        values_in.shape[:-1] + (feature_count * feature_count,)
    )
    constant = jnp.ones(values_in.shape[:-1] + (1,), jnp.float32)
    linear = values_in * feature_count ** (-0.25)
    quadratic = squares * (0.5**0.5 / feature_count**0.5)
    return jnp.concatenate([constant, linear, quadratic], axis=-1).astype(jnp.bfloat16)


def feature_columns(values_in):
    feature_count = values_in.shape[-2]
    length = values_in.shape[-1]
    squares = (values_in[..., :, None, :] * values_in[..., None, :, :]).reshape(
        values_in.shape[:-2] + (feature_count * feature_count, length)
    )
    constant = jnp.ones(values_in.shape[:-2] + (1, length), jnp.float32)
    linear = values_in * feature_count ** (-0.25)
    quadratic = squares * (0.5**0.5 / feature_count**0.5)
    return jnp.concatenate([constant, linear, quadratic], axis=-2).astype(jnp.bfloat16)


def gather_by_shifts(x, axis, n):
    me = lax.axis_index(axis)
    got = [x] + [lax.ppermute(x, axis, [(i, (i + k) % n) for i in range(n)]) for k in range(1, n)]
    stacked = jnp.stack(got)
    return jnp.take(stacked, (me - jnp.arange(n)) % n, axis=0)


def reduce_scatter_by_shifts(x, axis, n):
    me = lax.axis_index(axis)
    m = x.shape[0] // n
    total = lax.dynamic_slice_in_dim(x, me * m, m).astype(jnp.float32)
    for k in range(1, n):
        part = lax.dynamic_slice_in_dim(x, ((me + k) % n) * m, m)
        total = total + lax.ppermute(part, axis, [(i, (i + k) % n) for i in range(n)]).astype(
            jnp.float32
        )
    return total


def shards(
    tokens, qkv_weight, out_weight, head_gain, prefix_keys, prefix_values, suffix_len, prefix_owner
):
    n_row = lax.psum(1, ROW)
    n_col = lax.psum(1, COL)
    heads_here = head_gain.shape[0] // HD
    row_here = lax.axis_index("x") * 2 + lax.axis_index("c")
    col_here = lax.axis_index("y") * 2 + lax.axis_index("zh")
    flat = ROW + COL
    perm = [(i * n_col + j, j * n_col + i) for i in range(n_row) for j in range(n_col)]

    pref_here = prefix_keys.shape[0]
    plen_here = prefix_keys.shape[2]
    feats_cached = feature_columns(
        prefix_keys.reshape(pref_here, heads_here, FEAT, plen_here).astype(jnp.float32)
    )
    values_cached = prefix_values.reshape(pref_here, heads_here, HD, plen_here)
    partial_state = jnp.einsum(
        "phet,phvt->phev", feats_cached, values_cached, preferred_element_type=jnp.float32
    )
    state_shape = partial_state.shape[1:]
    piece = partial_state[0].size // n_col
    pieces = partial_state.astype(jnp.bfloat16).reshape(pref_here, n_col, piece)
    pieces = jnp.swapaxes(pieces, 0, 1).reshape(n_col, pref_here * piece)
    meta = jnp.stack([prefix_owner[0], suffix_len[0] // 16, suffix_len[0] % 16])
    meta = jnp.broadcast_to(meta.astype(jnp.bfloat16)[None], (n_col, 3))
    got = lax.all_to_all(jnp.concatenate([pieces, meta], axis=1), COL, 0, 0, tiled=True)
    meta = got[:, pref_here * piece :].astype(jnp.int32)
    owners = meta[:, 0]
    lens = meta[:, 1] * 16 + meta[:, 2]
    pieces = got[:, : pref_here * piece].reshape(n_col, pref_here, piece)
    pieces = jnp.sum(pieces.astype(jnp.float32), axis=0).astype(jnp.bfloat16)
    n_req = lax.psum(1, "req")
    pieces = jnp.broadcast_to(pieces[None], (n_req,) + pieces.shape)
    pieces = lax.all_to_all(pieces, "req", 0, 0, tiled=True)
    pieces = pieces.reshape((-1, piece))
    to_send = jnp.take(pieces, owners, axis=0)
    chosen = lax.all_to_all(to_send, COL, 0, 0, tiled=True)
    chosen = lax.ppermute(chosen, flat, perm)
    chosen = chosen.reshape(state_shape).astype(jnp.float32)

    both = jnp.concatenate([qkv_weight, out_weight], axis=1)
    both = lax.all_gather(both, ROW, axis=1, tiled=True)
    both = jnp.swapaxes(both.reshape(both.shape[0], n_row, -1), 0, 1)
    weight_all = both[:, :, : qkv_weight.shape[1]]
    out_w = both[:, :, qkv_weight.shape[1] :]
    partial_proj = jnp.einsum(
        "kdj,dt->kjt", weight_all, tokens, preferred_element_type=jnp.float32
    ).astype(jnp.bfloat16)
    partial_proj = partial_proj.reshape(-1, tokens.shape[1])
    partial_proj, to_send = lax.optimization_barrier((partial_proj, to_send))
    projected = reduce_scatter_by_shifts(partial_proj, "y", n_col // 2).astype(jnp.bfloat16)
    projected, chosen = lax.optimization_barrier((projected, chosen))
    projected = reduce_scatter_by_shifts(projected, "zh", 2).astype(jnp.bfloat16)
    projected = projected.T.reshape(SLOTS, heads_here, 2 * FEAT + HD)
    queries = projected[..., :FEAT]
    keys_now = projected[..., FEAT : 2 * FEAT]
    values_now = projected[..., 2 * FEAT :]

    feats_query = feature_map(queries.astype(jnp.float32)).astype(jnp.float32)
    carried = jnp.einsum("the,hev->thv", feats_query, chosen, precision=lax.Precision.HIGHEST)
    scores = jnp.einsum("thf,shf->hts", queries, keys_now, preferred_element_type=jnp.float32)
    weights = 1.0 + scores * FEAT ** (-0.5) + scores * scores * (0.5 / FEAT)
    positions = jnp.arange(SLOTS, dtype=jnp.int32)
    length = lens[row_here]
    allowed = (positions[None, :] <= positions[:, None]) & (positions[None, :] < length)
    weights = jnp.where(allowed[None], weights, 0.0).astype(jnp.bfloat16)
    within = jnp.einsum("hts,shv->thv", weights, values_now, preferred_element_type=jnp.float32)
    active = (positions < length)[:, None, None]
    attended = jnp.where(active, carried + within, 0.0)
    inverse_rms = lax.rsqrt(jnp.mean(attended * attended, axis=-1, keepdims=True) + epsilon)
    gains = lax.ppermute(head_gain, flat, perm).reshape(heads_here, HD)
    normed = (attended * inverse_rms * gains).astype(jnp.bfloat16).reshape(SLOTS, heads_here * HD)
    hidden = gather_by_shifts(gather_by_shifts(normed, "zh", 2), "y", n_col // 2)
    hidden = hidden.reshape((n_col,) + normed.shape)
    blocks = jnp.einsum("ktd,kde->ket", hidden, out_w, preferred_element_type=jnp.float32)
    mixed_sums = jnp.sum(blocks.astype(jnp.bfloat16).astype(jnp.float32), axis=0)
    return (tokens.astype(jnp.float32) + mixed_sums).astype(jnp.bfloat16)


def solution(mesh):
    n_req, n_row, n_col = (mesh.shape[a] for a in ("req", "row", "col"))
    fine = Mesh(
        np.asarray(mesh.devices).reshape(n_req, n_row // 2, 2, n_col // 2, 2),
        ("req", "x", "c", "y", "zh"),
    )
    in_specs = (
        P(COL, ("req",) + ROW),
        P(COL, ROW),
        P(ROW, COL),
        P(ROW),
        P("req", ROW, COL),
        P("req", ROW, COL),
        P(("req",) + COL),
        P(("req",) + COL),
    )
    out_specs = P(COL, ("req",) + ROW)
    return jax.shard_map(shards, mesh=fine, in_specs=in_specs, out_specs=out_specs, check_vma=False)
```

```python
import jax
import jax.numpy as jnp
import numpy as np
from jax import lax
from jax.sharding import Mesh, PartitionSpec as P

FEAT = 16
SLOTS = 512
HD = 112

ROW = ("x", "c")
COL = ("y", "zh")

epsilon = 1e-05


def feature_map(values_in):
    feature_count = values_in.shape[-1]
    squares = (values_in[..., :, None] * values_in[..., None, :]).reshape(
        values_in.shape[:-1] + (feature_count * feature_count,)
    )
    constant = jnp.ones(values_in.shape[:-1] + (1,), jnp.float32)
    linear = values_in * feature_count ** (-0.25)
    quadratic = squares * (0.5**0.5 / feature_count**0.5)
    return jnp.concatenate([constant, linear, quadratic], axis=-1).astype(jnp.bfloat16)


def feature_columns(values_in):
    feature_count = values_in.shape[-2]
    length = values_in.shape[-1]
    squares = (values_in[..., :, None, :] * values_in[..., None, :, :]).reshape(
        values_in.shape[:-2] + (feature_count * feature_count, length)
    )
    constant = jnp.ones(values_in.shape[:-2] + (1, length), jnp.float32)
    linear = values_in * feature_count ** (-0.25)
    quadratic = squares * (0.5**0.5 / feature_count**0.5)
    return jnp.concatenate([constant, linear, quadratic], axis=-2).astype(jnp.bfloat16)


def gather_by_shifts(x, axis, n):
    me = lax.axis_index(axis)
    got = [x] + [lax.ppermute(x, axis, [(i, (i + k) % n) for i in range(n)]) for k in range(1, n)]
    stacked = jnp.stack(got)
    return jnp.take(stacked, (me - jnp.arange(n)) % n, axis=0)


def reduce_scatter_by_shifts(x, axis, n):
    me = lax.axis_index(axis)
    m = x.shape[0] // n
    total = lax.dynamic_slice_in_dim(x, me * m, m).astype(jnp.float32)
    for k in range(1, n):
        part = lax.dynamic_slice_in_dim(x, ((me + k) % n) * m, m)
        total = total + lax.ppermute(part, axis, [(i, (i + k) % n) for i in range(n)]).astype(
            jnp.float32
        )
    return total


def shards(
    tokens, qkv_weight, out_weight, head_gain, prefix_keys, prefix_values, suffix_len, prefix_owner
):
    n_row = lax.psum(1, ROW)
    n_col = lax.psum(1, COL)
    heads_here = head_gain.shape[0] // HD
    row_here = lax.axis_index("x") * 2 + lax.axis_index("c")
    col_here = lax.axis_index("y") * 2 + lax.axis_index("zh")
    flat = ROW + COL
    perm = [(i * n_col + j, j * n_col + i) for i in range(n_row) for j in range(n_col)]

    pref_here = prefix_keys.shape[0]
    plen_here = prefix_keys.shape[2]
    feats_cached = feature_columns(
        prefix_keys.reshape(pref_here, heads_here, FEAT, plen_here).astype(jnp.float32)
    )
    values_cached = prefix_values.reshape(pref_here, heads_here, HD, plen_here)
    partial_state = jnp.einsum(
        "phet,phvt->phev", feats_cached, values_cached, preferred_element_type=jnp.float32
    )
    state_shape = partial_state.shape[1:]
    piece = partial_state[0].size // n_col
    pieces = partial_state.astype(jnp.bfloat16).reshape(pref_here, n_col, piece)
    pieces = jnp.swapaxes(pieces, 0, 1).reshape(n_col, pref_here * piece)
    meta = jnp.stack([prefix_owner[0], suffix_len[0] // 16, suffix_len[0] % 16])
    meta = jnp.broadcast_to(meta.astype(jnp.bfloat16)[None], (n_col, 3))
    got = lax.all_to_all(jnp.concatenate([pieces, meta], axis=1), COL, 0, 0, tiled=True)
    meta = got[:, pref_here * piece :].astype(jnp.int32)
    owners = meta[:, 0]
    lens = meta[:, 1] * 16 + meta[:, 2]
    pieces = got[:, : pref_here * piece].reshape(n_col, pref_here, piece)
    pieces = jnp.sum(pieces.astype(jnp.float32), axis=0).astype(jnp.bfloat16)
    n_req = lax.psum(1, "req")
    pieces = jnp.broadcast_to(pieces[None], (n_req,) + pieces.shape)
    pieces = lax.all_to_all(pieces, "req", 0, 0, tiled=True)
    pieces = pieces.reshape((-1, piece))
    to_send = jnp.take(pieces, owners, axis=0)
    chosen = lax.all_to_all(to_send, COL, 0, 0, tiled=True)
    chosen = lax.ppermute(chosen, flat, perm)
    chosen = chosen.reshape(state_shape).astype(jnp.float32)

    weight_all = gather_by_shifts(gather_by_shifts(qkv_weight, "c", 2), "x", n_row // 2)
    weight_all = weight_all.reshape((n_row,) + qkv_weight.shape)
    partial_proj = jnp.einsum(
        "kdj,dt->kjt", weight_all, tokens, preferred_element_type=jnp.float32
    ).astype(jnp.bfloat16)
    partial_proj = partial_proj.reshape(-1, tokens.shape[1])
    partial_proj, to_send = lax.optimization_barrier((partial_proj, to_send))
    projected = reduce_scatter_by_shifts(partial_proj, "y", n_col // 2).astype(jnp.bfloat16)
    projected, chosen = lax.optimization_barrier((projected, chosen))
    projected = reduce_scatter_by_shifts(projected, "zh", 2).astype(jnp.bfloat16)
    projected = projected.T.reshape(SLOTS, heads_here, 2 * FEAT + HD)
    queries = projected[..., :FEAT]
    keys_now = projected[..., FEAT : 2 * FEAT]
    values_now = projected[..., 2 * FEAT :]

    feats_query = feature_map(queries.astype(jnp.float32)).astype(jnp.float32)
    carried = jnp.einsum("the,hev->thv", feats_query, chosen, precision=lax.Precision.HIGHEST)
    scores = jnp.einsum("thf,shf->hts", queries, keys_now, preferred_element_type=jnp.float32)
    weights = 1.0 + scores * FEAT ** (-0.5) + scores * scores * (0.5 / FEAT)
    positions = jnp.arange(SLOTS, dtype=jnp.int32)
    length = lens[row_here]
    allowed = (positions[None, :] <= positions[:, None]) & (positions[None, :] < length)
    weights = jnp.where(allowed[None], weights, 0.0).astype(jnp.bfloat16)
    within = jnp.einsum("hts,shv->thv", weights, values_now, preferred_element_type=jnp.float32)
    active = (positions < length)[:, None, None]
    attended = jnp.where(active, carried + within, 0.0)
    inverse_rms = lax.rsqrt(jnp.mean(attended * attended, axis=-1, keepdims=True) + epsilon)
    gains = lax.ppermute(head_gain, flat, perm).reshape(heads_here, HD)
    normed = (attended * inverse_rms * gains).astype(jnp.bfloat16).reshape(SLOTS, heads_here * HD)
    hidden = gather_by_shifts(gather_by_shifts(normed, "zh", 2), "y", n_col // 2)
    hidden = hidden.reshape((n_col,) + normed.shape)
    out_weight, normed = lax.optimization_barrier((out_weight, normed))
    out_w = gather_by_shifts(gather_by_shifts(out_weight, "c", 2), "x", n_row // 2)
    out_w = out_w.reshape((n_row,) + out_weight.shape)
    blocks = jnp.einsum("ktd,kde->ket", hidden, out_w, preferred_element_type=jnp.float32)
    mixed_sums = jnp.sum(blocks.astype(jnp.bfloat16).astype(jnp.float32), axis=0)
    return (tokens.astype(jnp.float32) + mixed_sums).astype(jnp.bfloat16)


def solution(mesh):
    n_req, n_row, n_col = (mesh.shape[a] for a in ("req", "row", "col"))
    fine = Mesh(
        np.asarray(mesh.devices).reshape(n_req, n_row // 2, 2, n_col // 2, 2),
        ("req", "x", "c", "y", "zh"),
    )
    in_specs = (
        P(COL, ("req",) + ROW),
        P(COL, ROW),
        P(ROW, COL),
        P(ROW),
        P("req", ROW, COL),
        P("req", ROW, COL),
        P(("req",) + COL),
        P(("req",) + COL),
    )
    out_specs = P(COL, ("req",) + ROW)
    return jax.shard_map(shards, mesh=fine, in_specs=in_specs, out_specs=out_specs, check_vma=False)
```

```python
import jax
import jax.numpy as jnp
import numpy as np
from jax import lax
from jax.sharding import Mesh, PartitionSpec as P

FEAT = 16
SLOTS = 512
HD = 112

ROW = ("x", "c")
COL = ("y", "zh")

epsilon = 1e-05


def feature_map(values_in):
    feature_count = values_in.shape[-1]
    squares = (values_in[..., :, None] * values_in[..., None, :]).reshape(
        values_in.shape[:-1] + (feature_count * feature_count,)
    )
    constant = jnp.ones(values_in.shape[:-1] + (1,), jnp.float32)
    linear = values_in * feature_count ** (-0.25)
    quadratic = squares * (0.5**0.5 / feature_count**0.5)
    return jnp.concatenate([constant, linear, quadratic], axis=-1).astype(jnp.bfloat16)


def feature_columns(values_in):
    feature_count = values_in.shape[-2]
    length = values_in.shape[-1]
    squares = (values_in[..., :, None, :] * values_in[..., None, :, :]).reshape(
        values_in.shape[:-2] + (feature_count * feature_count, length)
    )
    constant = jnp.ones(values_in.shape[:-2] + (1, length), jnp.float32)
    linear = values_in * feature_count ** (-0.25)
    quadratic = squares * (0.5**0.5 / feature_count**0.5)
    return jnp.concatenate([constant, linear, quadratic], axis=-2).astype(jnp.bfloat16)


def gather_by_shifts(x, axis, n):
    me = lax.axis_index(axis)
    got = [x] + [lax.ppermute(x, axis, [(i, (i + k) % n) for i in range(n)]) for k in range(1, n)]
    stacked = jnp.stack(got)
    return jnp.take(stacked, (me - jnp.arange(n)) % n, axis=0)


def reduce_scatter_by_shifts(x, axis, n):
    me = lax.axis_index(axis)
    m = x.shape[0] // n
    total = lax.dynamic_slice_in_dim(x, me * m, m).astype(jnp.float32)
    for k in range(1, n):
        part = lax.dynamic_slice_in_dim(x, ((me + k) % n) * m, m)
        total = total + lax.ppermute(part, axis, [(i, (i + k) % n) for i in range(n)]).astype(
            jnp.float32
        )
    return total


def shards(
    tokens, qkv_weight, out_weight, head_gain, prefix_keys, prefix_values, suffix_len, prefix_owner
):
    n_row = lax.psum(1, ROW)
    n_col = lax.psum(1, COL)
    heads_here = head_gain.shape[0] // HD
    row_here = lax.axis_index("x") * 2 + lax.axis_index("c")
    col_here = lax.axis_index("y") * 2 + lax.axis_index("zh")
    flat = ROW + COL
    perm = [(i * n_col + j, j * n_col + i) for i in range(n_row) for j in range(n_col)]

    pref_here = prefix_keys.shape[0]
    plen_here = prefix_keys.shape[2]
    feats_cached = feature_columns(
        prefix_keys.reshape(pref_here, heads_here, FEAT, plen_here).astype(jnp.float32)
    )
    values_cached = prefix_values.reshape(pref_here, heads_here, HD, plen_here)
    partial_state = jnp.einsum(
        "phet,phvt->phev", feats_cached, values_cached, preferred_element_type=jnp.float32
    )
    state_shape = partial_state.shape[1:]
    piece = partial_state[0].size // n_col
    n_y = n_col // 2
    width = pref_here * piece
    pieces = partial_state.astype(jnp.bfloat16).reshape(pref_here, n_col, piece)
    pieces = jnp.swapaxes(pieces, 0, 1).reshape(n_y, 2, width)
    meta = jnp.stack([prefix_owner[0], suffix_len[0] // 16, suffix_len[0] % 16])
    meta = jnp.broadcast_to(meta.astype(jnp.bfloat16)[None, None], (n_y, 2, 3))
    got = lax.all_to_all(jnp.concatenate([pieces, meta], axis=2), "y", 0, 0, tiled=True)
    meta_y = got[:, 0, width:]
    half = jnp.sum(got[:, :, :width].astype(jnp.float32), axis=0).astype(jnp.bfloat16)
    zh_here = lax.axis_index("zh")
    mine = lax.dynamic_index_in_dim(half, zh_here, keepdims=False)
    other = lax.dynamic_index_in_dim(half, 1 - zh_here, keepdims=False)
    recv = lax.ppermute(
        jnp.concatenate([other, meta_y.reshape(-1)]), "zh", [(0, 1), (1, 0)]
    )
    pieces = (mine.astype(jnp.float32) + recv[:width].astype(jnp.float32)).astype(jnp.bfloat16)
    pieces = pieces.reshape(pref_here, piece)
    meta_other = recv[width:].reshape(n_y, 3)
    meta = jnp.where(
        zh_here == 0,
        jnp.stack([meta_y, meta_other], axis=1),
        jnp.stack([meta_other, meta_y], axis=1),
    ).reshape(n_col, 3).astype(jnp.int32)
    owners = meta[:, 0]
    lens = meta[:, 1] * 16 + meta[:, 2]
    n_req = lax.psum(1, "req")
    pieces = jnp.broadcast_to(pieces[None], (n_req,) + pieces.shape)
    pieces = lax.all_to_all(pieces, "req", 0, 0, tiled=True)
    pieces = pieces.reshape((-1, piece))
    to_send = jnp.take(pieces, owners, axis=0)
    chosen = lax.all_to_all(to_send, COL, 0, 0, tiled=True)
    chosen = lax.ppermute(chosen, flat, perm)
    chosen = chosen.reshape(state_shape).astype(jnp.float32)

    weight_all = gather_by_shifts(gather_by_shifts(qkv_weight, "c", 2), "x", n_row // 2)
    weight_all = weight_all.reshape((n_row,) + qkv_weight.shape)
    partial_proj = jnp.einsum(
        "kdj,dt->kjt", weight_all, tokens, preferred_element_type=jnp.float32
    ).astype(jnp.bfloat16)
    partial_proj = partial_proj.reshape(-1, tokens.shape[1])
    partial_proj, to_send = lax.optimization_barrier((partial_proj, to_send))
    projected = reduce_scatter_by_shifts(partial_proj, "y", n_col // 2).astype(jnp.bfloat16)
    projected, chosen = lax.optimization_barrier((projected, chosen))
    projected = reduce_scatter_by_shifts(projected, "zh", 2).astype(jnp.bfloat16)
    projected = projected.T.reshape(SLOTS, heads_here, 2 * FEAT + HD)
    queries = projected[..., :FEAT]
    keys_now = projected[..., FEAT : 2 * FEAT]
    values_now = projected[..., 2 * FEAT :]

    feats_query = feature_map(queries.astype(jnp.float32)).astype(jnp.float32)
    carried = jnp.einsum("the,hev->thv", feats_query, chosen, precision=lax.Precision.HIGHEST)
    scores = jnp.einsum("thf,shf->hts", queries, keys_now, preferred_element_type=jnp.float32)
    weights = 1.0 + scores * FEAT ** (-0.5) + scores * scores * (0.5 / FEAT)
    positions = jnp.arange(SLOTS, dtype=jnp.int32)
    length = lens[row_here]
    allowed = (positions[None, :] <= positions[:, None]) & (positions[None, :] < length)
    weights = jnp.where(allowed[None], weights, 0.0).astype(jnp.bfloat16)
    within = jnp.einsum("hts,shv->thv", weights, values_now, preferred_element_type=jnp.float32)
    active = (positions < length)[:, None, None]
    attended = jnp.where(active, carried + within, 0.0)
    inverse_rms = lax.rsqrt(jnp.mean(attended * attended, axis=-1, keepdims=True) + epsilon)
    gains = lax.ppermute(head_gain, flat, perm).reshape(heads_here, HD)
    normed = (attended * inverse_rms * gains).astype(jnp.bfloat16).reshape(SLOTS, heads_here * HD)
    hidden = gather_by_shifts(gather_by_shifts(normed, "zh", 2), "y", n_col // 2)
    hidden = hidden.reshape((n_col,) + normed.shape)
    out_w = gather_by_shifts(gather_by_shifts(out_weight, "c", 2), "x", n_row // 2)
    out_w = out_w.reshape((n_row,) + out_weight.shape)
    blocks = jnp.einsum("ktd,kde->ket", hidden, out_w, preferred_element_type=jnp.float32)
    mixed_sums = jnp.sum(blocks.astype(jnp.bfloat16).astype(jnp.float32), axis=0)
    return (tokens.astype(jnp.float32) + mixed_sums).astype(jnp.bfloat16)


def solution(mesh):
    n_req, n_row, n_col = (mesh.shape[a] for a in ("req", "row", "col"))
    fine = Mesh(
        np.asarray(mesh.devices).reshape(n_req, n_row // 2, 2, n_col // 2, 2),
        ("req", "x", "c", "y", "zh"),
    )
    in_specs = (
        P(COL, ("req",) + ROW),
        P(COL, ROW),
        P(ROW, COL),
        P(ROW),
        P("req", ROW, COL),
        P("req", ROW, COL),
        P(("req",) + COL),
        P(("req",) + COL),
    )
    out_specs = P(COL, ("req",) + ROW)
    return jax.shard_map(shards, mesh=fine, in_specs=in_specs, out_specs=out_specs, check_vma=False)
```

```python
import jax
import jax.numpy as jnp
import numpy as np
from jax import lax
from jax.sharding import Mesh, PartitionSpec as P

FEAT = 16
SLOTS = 512
HD = 112

ROW = ("x", "c")
COL = ("y", "zh")

epsilon = 1e-05


def feature_map(values_in):
    feature_count = values_in.shape[-1]
    squares = (values_in[..., :, None] * values_in[..., None, :]).reshape(
        values_in.shape[:-1] + (feature_count * feature_count,)
    )
    constant = jnp.ones(values_in.shape[:-1] + (1,), jnp.float32)
    linear = values_in * feature_count ** (-0.25)
    quadratic = squares * (0.5**0.5 / feature_count**0.5)
    return jnp.concatenate([constant, linear, quadratic], axis=-1).astype(jnp.bfloat16)


def feature_columns(values_in):
    feature_count = values_in.shape[-2]
    length = values_in.shape[-1]
    squares = (values_in[..., :, None, :] * values_in[..., None, :, :]).reshape(
        values_in.shape[:-2] + (feature_count * feature_count, length)
    )
    constant = jnp.ones(values_in.shape[:-2] + (1, length), jnp.float32)
    linear = values_in * feature_count ** (-0.25)
    quadratic = squares * (0.5**0.5 / feature_count**0.5)
    return jnp.concatenate([constant, linear, quadratic], axis=-2).astype(jnp.bfloat16)


def gather_by_shifts(x, axis, n):
    me = lax.axis_index(axis)
    got = [x] + [lax.ppermute(x, axis, [(i, (i + k) % n) for i in range(n)]) for k in range(1, n)]
    stacked = jnp.stack(got)
    return jnp.take(stacked, (me - jnp.arange(n)) % n, axis=0)


def reduce_scatter_by_shifts(x, axis, n):
    me = lax.axis_index(axis)
    m = x.shape[0] // n
    total = lax.dynamic_slice_in_dim(x, me * m, m).astype(jnp.float32)
    for k in range(1, n):
        part = lax.dynamic_slice_in_dim(x, ((me + k) % n) * m, m)
        total = total + lax.ppermute(part, axis, [(i, (i + k) % n) for i in range(n)]).astype(
            jnp.float32
        )
    return total


def shards(
    tokens, qkv_weight, out_weight, head_gain, prefix_keys, prefix_values, suffix_len, prefix_owner
):
    n_row = lax.psum(1, ROW)
    n_col = lax.psum(1, COL)
    heads_here = head_gain.shape[0] // HD
    row_here = lax.axis_index("x") * 2 + lax.axis_index("c")
    col_here = lax.axis_index("y") * 2 + lax.axis_index("zh")
    flat = ROW + COL
    perm = [(i * n_col + j, j * n_col + i) for i in range(n_row) for j in range(n_col)]

    pref_here = prefix_keys.shape[0]
    plen_here = prefix_keys.shape[2]
    feats_cached = feature_columns(
        prefix_keys.reshape(pref_here, heads_here, FEAT, plen_here).astype(jnp.float32)
    )
    values_cached = prefix_values.reshape(pref_here, heads_here, HD, plen_here)
    partial_state = jnp.einsum(
        "phet,phvt->phev", feats_cached, values_cached, preferred_element_type=jnp.float32
    )
    state_shape = partial_state.shape[1:]
    piece = partial_state[0].size // n_col
    n_y = n_col // 2
    width = pref_here * piece
    pieces = partial_state.astype(jnp.bfloat16).reshape(pref_here, n_col, piece)
    pieces = jnp.swapaxes(pieces, 0, 1).reshape(n_y, 2, width)
    meta = jnp.stack([prefix_owner[0], suffix_len[0] // 16, suffix_len[0] % 16])
    meta = jnp.broadcast_to(meta.astype(jnp.bfloat16)[None, None], (n_y, 2, 3))
    got = lax.all_to_all(jnp.concatenate([pieces, meta], axis=2), "y", 0, 0, tiled=True)
    meta_y = got[:, 0, width:]
    half = jnp.sum(got[:, :, :width].astype(jnp.float32), axis=0).astype(jnp.bfloat16)
    zh_here = lax.axis_index("zh")
    mine = lax.dynamic_index_in_dim(half, zh_here, keepdims=False)
    other = lax.dynamic_index_in_dim(half, 1 - zh_here, keepdims=False)
    recv = lax.ppermute(
        jnp.concatenate([other, meta_y.reshape(-1)]), "zh", [(0, 1), (1, 0)]
    )
    pieces = (mine.astype(jnp.float32) + recv[:width].astype(jnp.float32)).astype(jnp.bfloat16)
    pieces = pieces.reshape(pref_here, piece)
    meta_other = recv[width:].reshape(n_y, 3)
    meta = jnp.where(
        zh_here == 0,
        jnp.stack([meta_y, meta_other], axis=1),
        jnp.stack([meta_other, meta_y], axis=1),
    ).reshape(n_col, 3).astype(jnp.int32)
    owners = meta[:, 0]
    lens = meta[:, 1] * 16 + meta[:, 2]
    n_req = lax.psum(1, "req")
    pieces = jnp.broadcast_to(pieces[None], (n_req,) + pieces.shape)
    pieces = lax.all_to_all(pieces, "req", 0, 0, tiled=True)
    pieces = pieces.reshape((-1, piece))
    to_send = jnp.take(pieces, owners, axis=0)
    chosen = lax.all_to_all(to_send, COL, 0, 0, tiled=True)
    chosen = lax.ppermute(chosen, flat, perm)
    chosen = chosen.reshape(state_shape).astype(jnp.float32)

    both = jnp.concatenate([qkv_weight, out_weight], axis=1)
    both = gather_by_shifts(gather_by_shifts(both, "c", 2), "x", n_row // 2)
    both = both.reshape((n_row,) + both.shape[2:])
    weight_all = both[:, :, : qkv_weight.shape[1]]
    out_w = both[:, :, qkv_weight.shape[1] :]
    partial_proj = jnp.einsum(
        "kdj,dt->kjt", weight_all, tokens, preferred_element_type=jnp.float32
    ).astype(jnp.bfloat16)
    partial_proj = partial_proj.reshape(-1, tokens.shape[1])
    partial_proj, to_send = lax.optimization_barrier((partial_proj, to_send))
    projected = reduce_scatter_by_shifts(partial_proj, "y", n_col // 2).astype(jnp.bfloat16)
    projected, chosen = lax.optimization_barrier((projected, chosen))
    projected = reduce_scatter_by_shifts(projected, "zh", 2).astype(jnp.bfloat16)
    projected = projected.T.reshape(SLOTS, heads_here, 2 * FEAT + HD)
    queries = projected[..., :FEAT]
    keys_now = projected[..., FEAT : 2 * FEAT]
    values_now = projected[..., 2 * FEAT :]

    feats_query = feature_map(queries.astype(jnp.float32)).astype(jnp.float32)
    carried = jnp.einsum("the,hev->thv", feats_query, chosen, precision=lax.Precision.HIGHEST)
    scores = jnp.einsum("thf,shf->hts", queries, keys_now, preferred_element_type=jnp.float32)
    weights = 1.0 + scores * FEAT ** (-0.5) + scores * scores * (0.5 / FEAT)
    positions = jnp.arange(SLOTS, dtype=jnp.int32)
    length = lens[row_here]
    allowed = (positions[None, :] <= positions[:, None]) & (positions[None, :] < length)
    weights = jnp.where(allowed[None], weights, 0.0).astype(jnp.bfloat16)
    within = jnp.einsum("hts,shv->thv", weights, values_now, preferred_element_type=jnp.float32)
    active = (positions < length)[:, None, None]
    attended = jnp.where(active, carried + within, 0.0)
    inverse_rms = lax.rsqrt(jnp.mean(attended * attended, axis=-1, keepdims=True) + epsilon)
    gains = lax.ppermute(head_gain, flat, perm).reshape(heads_here, HD)
    normed = (attended * inverse_rms * gains).astype(jnp.bfloat16).reshape(SLOTS, heads_here * HD)
    hidden = gather_by_shifts(gather_by_shifts(normed, "zh", 2), "y", n_col // 2)
    hidden = hidden.reshape((n_col,) + normed.shape)
    blocks = jnp.einsum("ktd,kde->ket", hidden, out_w, preferred_element_type=jnp.float32)
    mixed_sums = jnp.sum(blocks.astype(jnp.bfloat16).astype(jnp.float32), axis=0)
    return (tokens.astype(jnp.float32) + mixed_sums).astype(jnp.bfloat16)


def solution(mesh):
    n_req, n_row, n_col = (mesh.shape[a] for a in ("req", "row", "col"))
    fine = Mesh(
        np.asarray(mesh.devices).reshape(n_req, n_row // 2, 2, n_col // 2, 2),
        ("req", "x", "c", "y", "zh"),
    )
    in_specs = (
        P(COL, ("req",) + ROW),
        P(COL, ROW),
        P(ROW, COL),
        P(ROW),
        P("req", ROW, COL),
        P("req", ROW, COL),
        P(("req",) + COL),
        P(("req",) + COL),
    )
    out_specs = P(COL, ("req",) + ROW)
    return jax.shard_map(shards, mesh=fine, in_specs=in_specs, out_specs=out_specs, check_vma=False)
```

```python
import jax
import jax.numpy as jnp
import numpy as np
from jax import lax
from jax.sharding import Mesh, PartitionSpec as P

FEAT = 16
SLOTS = 512
HD = 112

ROW = ("x", "c")
COL = ("y", "zh")

epsilon = 1e-05


def feature_map(values_in):
    feature_count = values_in.shape[-1]
    squares = (values_in[..., :, None] * values_in[..., None, :]).reshape(
        values_in.shape[:-1] + (feature_count * feature_count,)
    )
    constant = jnp.ones(values_in.shape[:-1] + (1,), jnp.float32)
    linear = values_in * feature_count ** (-0.25)
    quadratic = squares * (0.5**0.5 / feature_count**0.5)
    return jnp.concatenate([constant, linear, quadratic], axis=-1).astype(jnp.bfloat16)


def feature_columns(values_in):
    feature_count = values_in.shape[-2]
    length = values_in.shape[-1]
    squares = (values_in[..., :, None, :] * values_in[..., None, :, :]).reshape(
        values_in.shape[:-2] + (feature_count * feature_count, length)
    )
    constant = jnp.ones(values_in.shape[:-2] + (1, length), jnp.float32)
    linear = values_in * feature_count ** (-0.25)
    quadratic = squares * (0.5**0.5 / feature_count**0.5)
    return jnp.concatenate([constant, linear, quadratic], axis=-2).astype(jnp.bfloat16)


def gather_by_shifts(x, axis, n):
    me = lax.axis_index(axis)
    got = [x] + [lax.ppermute(x, axis, [(i, (i + k) % n) for i in range(n)]) for k in range(1, n)]
    stacked = jnp.stack(got)
    return jnp.take(stacked, (me - jnp.arange(n)) % n, axis=0)


def reduce_scatter_by_shifts(x, axis, n):
    me = lax.axis_index(axis)
    m = x.shape[0] // n
    total = lax.dynamic_slice_in_dim(x, me * m, m).astype(jnp.float32)
    for k in range(1, n):
        part = lax.dynamic_slice_in_dim(x, ((me + k) % n) * m, m)
        total = total + lax.ppermute(part, axis, [(i, (i + k) % n) for i in range(n)]).astype(
            jnp.float32
        )
    return total


def shards(
    tokens, qkv_weight, out_weight, head_gain, prefix_keys, prefix_values, suffix_len, prefix_owner
):
    n_row = lax.psum(1, ROW)
    n_col = lax.psum(1, COL)
    heads_here = head_gain.shape[0] // HD
    row_here = lax.axis_index("x") * 2 + lax.axis_index("c")
    col_here = lax.axis_index("y") * 2 + lax.axis_index("zh")
    flat = ROW + COL
    perm = [(i * n_col + j, j * n_col + i) for i in range(n_row) for j in range(n_col)]

    pref_here = prefix_keys.shape[0]
    plen_here = prefix_keys.shape[2]
    feats_cached = feature_columns(
        prefix_keys.reshape(pref_here, heads_here, FEAT, plen_here).astype(jnp.float32)
    )
    values_cached = prefix_values.reshape(pref_here, heads_here, HD, plen_here)
    partial_state = jnp.einsum(
        "phet,phvt->phev", feats_cached, values_cached, preferred_element_type=jnp.float32
    )
    state_shape = partial_state.shape[1:]
    piece = partial_state[0].size // n_col
    n_y = n_col // 2
    width = pref_here * piece
    pieces = partial_state.astype(jnp.bfloat16).reshape(pref_here, n_col, piece)
    pieces = jnp.swapaxes(pieces, 0, 1).reshape(n_y, 2, width)
    meta = jnp.stack([prefix_owner[0], suffix_len[0] // 16, suffix_len[0] % 16])
    meta = jnp.broadcast_to(meta.astype(jnp.bfloat16)[None, None], (n_y, 2, 3))
    got = lax.all_to_all(jnp.concatenate([pieces, meta], axis=2), "y", 0, 0, tiled=True)
    meta_y = got[:, 0, width:]
    half = jnp.sum(got[:, :, :width].astype(jnp.float32), axis=0).astype(jnp.bfloat16)
    zh_here = lax.axis_index("zh")
    mine = lax.dynamic_index_in_dim(half, zh_here, keepdims=False)
    other = lax.dynamic_index_in_dim(half, 1 - zh_here, keepdims=False)
    recv = lax.ppermute(
        jnp.concatenate([other, meta_y.reshape(-1)]), "zh", [(0, 1), (1, 0)]
    )
    pieces = (mine.astype(jnp.float32) + recv[:width].astype(jnp.float32)).astype(jnp.bfloat16)
    pieces = pieces.reshape(pref_here, piece)
    meta_other = recv[width:].reshape(n_y, 3)
    meta = jnp.where(
        zh_here == 0,
        jnp.stack([meta_y, meta_other], axis=1),
        jnp.stack([meta_other, meta_y], axis=1),
    ).reshape(n_col, 3).astype(jnp.int32)
    owners = meta[:, 0]
    lens = meta[:, 1] * 16 + meta[:, 2]
    n_req = lax.psum(1, "req")
    pieces = jnp.broadcast_to(pieces[None], (n_req,) + pieces.shape)
    pieces = lax.all_to_all(pieces, "req", 0, 0, tiled=True)
    pieces = pieces.reshape((-1, piece))
    to_send = jnp.take(pieces, owners, axis=0)
    chosen = lax.all_to_all(to_send, COL, 0, 0, tiled=True)
    chosen = lax.ppermute(chosen, flat, perm)
    chosen = chosen.reshape(state_shape).astype(jnp.float32)

    both = jnp.concatenate([qkv_weight, out_weight], axis=1)
    both = gather_by_shifts(gather_by_shifts(both, "c", 2), "x", n_row // 2)
    both = both.reshape((n_row,) + both.shape[2:])
    weight_all = both[:, :, : qkv_weight.shape[1]]
    out_w = both[:, :, qkv_weight.shape[1] :]
    partial_proj = jnp.einsum(
        "kdj,dt->kjt", weight_all, tokens, preferred_element_type=jnp.float32
    ).astype(jnp.bfloat16)
    partial_proj = partial_proj.reshape(-1, tokens.shape[1])
    partial_proj, to_send = lax.optimization_barrier((partial_proj, to_send))
    projected = reduce_scatter_by_shifts(partial_proj, "y", n_col // 2).astype(jnp.bfloat16)
    projected, chosen = lax.optimization_barrier((projected, chosen))
    projected = reduce_scatter_by_shifts(projected, "zh", 2).astype(jnp.bfloat16)
    projected = projected.T.reshape(SLOTS, heads_here, 2 * FEAT + HD)
    queries = projected[..., :FEAT]
    keys_now = projected[..., FEAT : 2 * FEAT]
    values_now = projected[..., 2 * FEAT :]

    feats_query = feature_map(queries.astype(jnp.float32)).astype(jnp.float32)
    carried = jnp.einsum("the,hev->thv", feats_query, chosen, precision=lax.Precision.HIGHEST)
    scores = jnp.einsum("thf,shf->hts", queries, keys_now, preferred_element_type=jnp.float32)
    weights = 1.0 + scores * FEAT ** (-0.5) + scores * scores * (0.5 / FEAT)
    positions = jnp.arange(SLOTS, dtype=jnp.int32)
    length = lens[row_here]
    allowed = (positions[None, :] <= positions[:, None]) & (positions[None, :] < length)
    weights = jnp.where(allowed[None], weights, 0.0).astype(jnp.bfloat16)
    within = jnp.einsum("hts,shv->thv", weights, values_now, preferred_element_type=jnp.float32)
    active = (positions < length)[:, None, None]
    attended = jnp.where(active, carried + within, 0.0)
    inverse_rms = lax.rsqrt(jnp.mean(attended * attended, axis=-1, keepdims=True) + epsilon)
    gains = lax.ppermute(head_gain, flat, perm).reshape(heads_here, HD)
    normed = (attended * inverse_rms * gains).astype(jnp.bfloat16).reshape(SLOTS, heads_here * HD)
    own_y = gather_by_shifts(normed, "y", n_col // 2)
    partner = lax.ppermute(normed, "zh", [(0, 1), (1, 0)])
    partner_y = gather_by_shifts(partner, "y", n_col // 2)
    zh_first = lax.axis_index("zh") == 0
    hidden = jnp.where(
        zh_first, jnp.stack([own_y, partner_y], axis=1), jnp.stack([partner_y, own_y], axis=1)
    )
    hidden = hidden.reshape((n_col,) + normed.shape)
    blocks = jnp.einsum("ktd,kde->ket", hidden, out_w, preferred_element_type=jnp.float32)
    mixed_sums = jnp.sum(blocks.astype(jnp.bfloat16).astype(jnp.float32), axis=0)
    return (tokens.astype(jnp.float32) + mixed_sums).astype(jnp.bfloat16)


def solution(mesh):
    n_req, n_row, n_col = (mesh.shape[a] for a in ("req", "row", "col"))
    fine = Mesh(
        np.asarray(mesh.devices).reshape(n_req, n_row // 2, 2, n_col // 2, 2),
        ("req", "x", "c", "y", "zh"),
    )
    in_specs = (
        P(COL, ("req",) + ROW),
        P(COL, ROW),
        P(ROW, COL),
        P(ROW),
        P("req", ROW, COL),
        P("req", ROW, COL),
        P(("req",) + COL),
        P(("req",) + COL),
    )
    out_specs = P(COL, ("req",) + ROW)
    return jax.shard_map(shards, mesh=fine, in_specs=in_specs, out_specs=out_specs, check_vma=False)
```

```python
import jax
import jax.numpy as jnp
import numpy as np
from jax import lax
from jax.sharding import Mesh, PartitionSpec as P

FEAT = 16
SLOTS = 512
HD = 112

ROW = ("x", "c")
COL = ("y", "zh")

epsilon = 1e-05


def feature_map(values_in):
    feature_count = values_in.shape[-1]
    squares = (values_in[..., :, None] * values_in[..., None, :]).reshape(
        values_in.shape[:-1] + (feature_count * feature_count,)
    )
    constant = jnp.ones(values_in.shape[:-1] + (1,), jnp.float32)
    linear = values_in * feature_count ** (-0.25)
    quadratic = squares * (0.5**0.5 / feature_count**0.5)
    return jnp.concatenate([constant, linear, quadratic], axis=-1).astype(jnp.bfloat16)


def feature_columns(values_in):
    feature_count = values_in.shape[-2]
    length = values_in.shape[-1]
    squares = (values_in[..., :, None, :] * values_in[..., None, :, :]).reshape(
        values_in.shape[:-2] + (feature_count * feature_count, length)
    )
    constant = jnp.ones(values_in.shape[:-2] + (1, length), jnp.float32)
    linear = values_in * feature_count ** (-0.25)
    quadratic = squares * (0.5**0.5 / feature_count**0.5)
    return jnp.concatenate([constant, linear, quadratic], axis=-2).astype(jnp.bfloat16)


def gather_by_shifts(x, axis, n):
    me = lax.axis_index(axis)
    got = [x] + [lax.ppermute(x, axis, [(i, (i + k) % n) for i in range(n)]) for k in range(1, n)]
    stacked = jnp.stack(got)
    return jnp.take(stacked, (me - jnp.arange(n)) % n, axis=0)


def reduce_scatter_by_shifts(x, axis, n):
    me = lax.axis_index(axis)
    m = x.shape[0] // n
    total = lax.dynamic_slice_in_dim(x, me * m, m).astype(jnp.float32)
    for k in range(1, n):
        part = lax.dynamic_slice_in_dim(x, ((me + k) % n) * m, m)
        total = total + lax.ppermute(part, axis, [(i, (i + k) % n) for i in range(n)]).astype(
            jnp.float32
        )
    return total


def shards(
    tokens, qkv_weight, out_weight, head_gain, prefix_keys, prefix_values, suffix_len, prefix_owner
):
    n_row = lax.psum(1, ROW)
    n_col = lax.psum(1, COL)
    heads_here = head_gain.shape[0] // HD
    row_here = lax.axis_index("x") * 2 + lax.axis_index("c")
    col_here = lax.axis_index("y") * 2 + lax.axis_index("zh")
    flat = ROW + COL
    perm = [(i * n_col + j, j * n_col + i) for i in range(n_row) for j in range(n_col)]

    pref_here = prefix_keys.shape[0]
    plen_here = prefix_keys.shape[2]
    feats_cached = feature_columns(
        prefix_keys.reshape(pref_here, heads_here, FEAT, plen_here).astype(jnp.float32)
    )
    values_cached = prefix_values.reshape(pref_here, heads_here, HD, plen_here)
    partial_state = jnp.einsum(
        "phet,phvt->phev", feats_cached, values_cached, preferred_element_type=jnp.float32
    )
    state_shape = partial_state.shape[1:]
    piece = partial_state[0].size // n_col
    n_y = n_col // 2
    width = pref_here * piece
    pieces = partial_state.astype(jnp.bfloat16).reshape(pref_here, n_col, piece)
    pieces = jnp.swapaxes(pieces, 0, 1).reshape(n_y, 2, width)
    meta = jnp.stack([prefix_owner[0], suffix_len[0] // 16, suffix_len[0] % 16])
    meta = jnp.broadcast_to(meta.astype(jnp.bfloat16)[None, None], (n_y, 2, 3))
    got = lax.all_to_all(jnp.concatenate([pieces, meta], axis=2), "y", 0, 0, tiled=True)
    meta_y = got[:, 0, width:]
    half = jnp.sum(got[:, :, :width].astype(jnp.float32), axis=0).astype(jnp.bfloat16)
    zh_here = lax.axis_index("zh")
    mine = lax.dynamic_index_in_dim(half, zh_here, keepdims=False)
    other = lax.dynamic_index_in_dim(half, 1 - zh_here, keepdims=False)
    recv = lax.ppermute(
        jnp.concatenate([other, meta_y.reshape(-1)]), "zh", [(0, 1), (1, 0)]
    )
    pieces = (mine.astype(jnp.float32) + recv[:width].astype(jnp.float32)).astype(jnp.bfloat16)
    pieces = pieces.reshape(pref_here, piece)
    meta_other = recv[width:].reshape(n_y, 3)
    meta = jnp.where(
        zh_here == 0,
        jnp.stack([meta_y, meta_other], axis=1),
        jnp.stack([meta_other, meta_y], axis=1),
    ).reshape(n_col, 3).astype(jnp.int32)
    owners = meta[:, 0]
    lens = meta[:, 1] * 16 + meta[:, 2]
    n_req = lax.psum(1, "req")
    pieces = jnp.broadcast_to(pieces[None], (n_req,) + pieces.shape)
    pieces = lax.all_to_all(pieces, "req", 0, 0, tiled=True)
    pieces = pieces.reshape((-1, piece))
    to_send = jnp.take(pieces, owners, axis=0)
    chosen = lax.all_to_all(to_send, COL, 0, 0, tiled=True)
    g_hi = lax.reduce_precision(head_gain, exponent_bits=8, mantissa_bits=7)
    g_rest = head_gain - g_hi
    g_mid = lax.reduce_precision(g_rest, exponent_bits=8, mantissa_bits=7)
    g_lo = lax.reduce_precision(g_rest - g_mid, exponent_bits=8, mantissa_bits=7)
    g_parts = jnp.concatenate([g_hi, g_mid, g_lo]).astype(jnp.bfloat16)
    n_state = chosen.size
    moved = lax.ppermute(jnp.concatenate([chosen.reshape(-1), g_parts]), flat, perm)
    chosen = moved[:n_state].reshape(chosen.shape)
    g_parts = moved[n_state:].reshape(3, -1).astype(jnp.float32)
    gains_moved = g_parts[0] + g_parts[1] + g_parts[2]
    chosen = chosen.reshape(state_shape).astype(jnp.float32)

    both = jnp.concatenate([qkv_weight, out_weight], axis=1)
    both = gather_by_shifts(gather_by_shifts(both, "c", 2), "x", n_row // 2)
    both = both.reshape((n_row,) + both.shape[2:])
    weight_all = both[:, :, : qkv_weight.shape[1]]
    out_w = both[:, :, qkv_weight.shape[1] :]
    partial_proj = jnp.einsum(
        "kdj,dt->kjt", weight_all, tokens, preferred_element_type=jnp.float32
    ).astype(jnp.bfloat16)
    partial_proj = partial_proj.reshape(-1, tokens.shape[1])
    partial_proj, to_send = lax.optimization_barrier((partial_proj, to_send))
    projected = reduce_scatter_by_shifts(partial_proj, "y", n_col // 2).astype(jnp.bfloat16)
    projected, chosen = lax.optimization_barrier((projected, chosen))
    projected = reduce_scatter_by_shifts(projected, "zh", 2).astype(jnp.bfloat16)
    projected = projected.T.reshape(SLOTS, heads_here, 2 * FEAT + HD)
    queries = projected[..., :FEAT]
    keys_now = projected[..., FEAT : 2 * FEAT]
    values_now = projected[..., 2 * FEAT :]

    feats_query = feature_map(queries.astype(jnp.float32)).astype(jnp.float32)
    carried = jnp.einsum("the,hev->thv", feats_query, chosen, precision=lax.Precision.HIGHEST)
    scores = jnp.einsum("thf,shf->hts", queries, keys_now, preferred_element_type=jnp.float32)
    weights = 1.0 + scores * FEAT ** (-0.5) + scores * scores * (0.5 / FEAT)
    positions = jnp.arange(SLOTS, dtype=jnp.int32)
    length = lens[row_here]
    allowed = (positions[None, :] <= positions[:, None]) & (positions[None, :] < length)
    weights = jnp.where(allowed[None], weights, 0.0).astype(jnp.bfloat16)
    within = jnp.einsum("hts,shv->thv", weights, values_now, preferred_element_type=jnp.float32)
    active = (positions < length)[:, None, None]
    attended = jnp.where(active, carried + within, 0.0)
    inverse_rms = lax.rsqrt(jnp.mean(attended * attended, axis=-1, keepdims=True) + epsilon)
    gains = gains_moved.reshape(heads_here, HD)
    normed = (attended * inverse_rms * gains).astype(jnp.bfloat16).reshape(SLOTS, heads_here * HD)
    hidden = gather_by_shifts(gather_by_shifts(normed, "zh", 2), "y", n_col // 2)
    hidden = hidden.reshape((n_col,) + normed.shape)
    blocks = jnp.einsum("ktd,kde->ket", hidden, out_w, preferred_element_type=jnp.float32)
    mixed_sums = jnp.sum(blocks.astype(jnp.bfloat16).astype(jnp.float32), axis=0)
    return (tokens.astype(jnp.float32) + mixed_sums).astype(jnp.bfloat16)


def solution(mesh):
    n_req, n_row, n_col = (mesh.shape[a] for a in ("req", "row", "col"))
    fine = Mesh(
        np.asarray(mesh.devices).reshape(n_req, n_row // 2, 2, n_col // 2, 2),
        ("req", "x", "c", "y", "zh"),
    )
    in_specs = (
        P(COL, ("req",) + ROW),
        P(COL, ROW),
        P(ROW, COL),
        P(ROW),
        P("req", ROW, COL),
        P("req", ROW, COL),
        P(("req",) + COL),
        P(("req",) + COL),
    )
    out_specs = P(COL, ("req",) + ROW)
    return jax.shard_map(shards, mesh=fine, in_specs=in_specs, out_specs=out_specs, check_vma=False)
```
